32 devices in a mesh: dp: 2 (over y), expert: 16 (over z, x, core).
Axes of the slice: x: 2, y: 2, z: 4, core: 2. Of those that a mesh axis runs over, the one named last changes fastest.
Arguments:
- tokens: bfloat16 [2048, 1024], P(('dp', 'expert')), may hold values from -6 to 6
- cotangent: bfloat16 [2048, 1024], P(('dp', 'expert')), may hold values from -6 to 6
- expert_ids: int32 [2048, 6], P(('dp', 'expert')), may hold values from 0 to 15, all different within a row; in each aligned block of 64 rows (0 to 63, 64 to 127, ...) at most 32 rows name the same one
- gate_probs: float32 [2048, 6], P(('dp', 'expert')), may hold values from 0.1 to 1
- w_gate_up: bfloat16 [16, 1024, 1408], P('expert', 'dp'), may hold values from -0.1875 to 0.1875
- w_down: bfloat16 [16, 704, 1024], P('expert'), may hold values from -0.21875 to 0.21875
Outputs:
- layer_out: bfloat16 [2048, 1024], P(('dp', 'expert'))
- input_grad: bfloat16 [2048, 1024], P(('dp', 'expert'))
- prob_grad: float32 [2048, 6], P(('dp', 'expert'))
- gate_up_grad: bfloat16 [16, 1024, 1408], P('expert', 'dp')
The draws below stay inside these ranges and needn't reach their ends.
Inputs may be any that keep to these rules, and one draw needn't show every extreme that they name: `expert_ids`: each row names 6 different experts. Within each aligned block of 64 rows no expert is named by more than 32 rows, and in some block an expert is named by exactly 32 rows.
All inputs are finite; a program needn't handle non-finite values.
Results may differ from the reference program's by a relative error of at most 0.013.
Values may be sent and summed in bfloat16 or wider, within the bound.
No kernel may reach another device: no remote copies, remote signals or barrier semaphores. Data moves between devices by JAX's collectives and lax.ppermute only.
A program may use at most 64 MiB of HBM per device.

```python
import math
import jax
import jax.numpy as jnp
import numpy as np
from jax import lax

D = 1024
FF = 704
TOP = 6
TOK_DEV = 64
EXPERTS = 16
REPLICAS = 2
CAP = 32
TOKENS = 2048


def block_levels(key, extent, pieces, least, top_value):
    def one(axis_at, parts):
        heights = jax.random.uniform(jax.random.fold_in(jax.random.fold_in(key, 6), axis_at), (parts,), jnp.float32, least / len(pieces), top_value / len(pieces))
        return jnp.repeat(jnp.exp(heights), extent[axis_at] // parts).reshape((-1,) + (1,) * (len(extent) - axis_at - 1))

    gain = one(*pieces[0])
    for cut in pieces[1:]:
        gain = gain * one(*cut)
    return gain


def assign_block(key, own, number, rows, count, top, bound, skew):
    ranking = jax.random.permutation(key, count)
    heavy_load, ordinary = shares(count, rows * top, bound, skew, True), shares(count, rows * top, bound, skew, False)
    places = jnp.arange(count)

    def named(tallies, turn):
        used = int((tallies > 0).sum())
        fixed = max(1, used // 4)
        passed = fixed + (places - fixed + turn * (used - fixed)) % max(1, count - fixed)
        return jnp.zeros((count,), jnp.int32).at[ranking[jnp.where(places < fixed, places, passed)]].set(jnp.asarray(tallies, jnp.int32))

    tallies = jnp.where(number % 4 == 0, named(heavy_load, number // 4), named(ordinary, number - number // 4 - 1))
    mixed = jax.random.permutation(jax.random.fold_in(own, 3), count)
    giver, sink = mixed[0:count // 2 * 2:2], mixed[1:count // 2 * 2:2]
    margin = jnp.minimum(tallies[giver] - 1, bound - tallies[sink]) // 2
    margin = jnp.where((giver == ranking[0]) | (sink == ranking[0]) | (tallies[sink] == 0), 0, jnp.maximum(margin, 0))
    passed = jax.random.randint(jax.random.fold_in(own, 4), (count // 2,), 0, 1 << 20) % (margin + 1)
    tallies = tallies.at[giver].add(-passed).at[sink].add(passed)
    members = jnp.searchsorted(jnp.cumsum(tallies), jnp.arange(rows * top), side="right").astype(jnp.int32)
    table = members.reshape(top, rows).T
    table = table[jax.random.permutation(jax.random.fold_in(own, 1), rows)]
    turn = jax.random.randint(jax.random.fold_in(own, 2), (rows, 1), 0, top)
    return jnp.take_along_axis(table, (jnp.arange(top)[None, :] + turn) % top, axis=1)


def shares(amount, total, bound, skew, full):
    portions = [(1 << 20) // math.isqrt(standing ** skew) + 1 for standing in range(1, amount + 1)]
    largest = bound if full else min(bound, max(-(-total // amount), total * portions[0] // sum(portions)))
    least = 1 if total - largest >= amount - 1 else 0
    holding, spare = [largest] + [least] * (amount - 1), total - largest - least * (amount - 1)
    while spare > 0:
        candidates = [i for i in range(1, amount) if holding[i] < largest] or [i for i in range(1, amount) if holding[i] < bound]
        whole, remaining = sum([portions[i] for i in candidates]), spare
        for i in candidates:
            addition = min(bound - holding[i], max(1, remaining * portions[i] // whole), spare)
            holding[i] = holding[i] + addition
            spare = spare - addition
    return np.array(holding)


def bell_draw(rng, extent, spread, bound, shards=(), kind=jnp.bfloat16):
    gain = block_levels(rng, extent, shards, -0.22, 0.18) if shards else 1.0
    drawn = jax.random.normal(rng, extent, jnp.float32) * spread * gain
    return jnp.minimum(jnp.maximum(drawn, -bound), bound).astype(kind)


def setup_inputs(seed: int = 0) -> dict:
    seeds = jax.random.split(jax.random.key(seed), 7)
    tokens = bell_draw(seeds[0], (TOKENS, D), 1.0, 6.0, ((0, 32),))
    cotangent = bell_draw(seeds[1], (TOKENS, D), 1.0, 6.0, ((0, 32),))
    expert_ids_keys = jax.random.split(jax.random.fold_in(seeds[2], 1), TOKENS // TOK_DEV)
    expert_ids_turns = jax.random.permutation(jax.random.fold_in(seeds[2], 3), TOKENS // TOK_DEV)
    expert_ids = jax.vmap(lambda own, number: assign_block(jax.random.fold_in(seeds[2], 2), own, number, TOK_DEV, EXPERTS, TOP, CAP, 2))(expert_ids_keys, expert_ids_turns).reshape((TOKENS, TOP))
    gate_probs = jnp.clip(jnp.exp(math.log(1.0) - 2.3025851 * jax.random.uniform(seeds[3], (TOKENS, TOP), jnp.float32) ** block_levels(seeds[3], (TOKENS, TOP), ((0, 32),), -0.2, 0.2)), 0.1, 1.0)
    w_gate_up = bell_draw(seeds[4], (EXPERTS, D, 2 * FF), D ** -0.5, 0.1875, ((0, 16), (1, 2)))
    w_down = bell_draw(seeds[5], (EXPERTS, FF, D), FF ** -0.5, 0.21875, ((0, 16),))
    return dict(tokens=tokens, cotangent=cotangent, expert_ids=expert_ids, gate_probs=gate_probs, w_gate_up=w_gate_up, w_down=w_down)


def place_slots(route_rows):
    onehot = (route_rows[:, :, None] == jnp.arange(EXPERTS, dtype=jnp.int32)[None, None, :]).astype(jnp.int32)
    before = jnp.cumsum(onehot, axis=1) - onehot
    return jnp.sum(before * onehot, axis=2).astype(jnp.int32)


def expert_pass(operands):
    input_rows, cot_rows, weight_pair, weight_down = operands
    gate_up = jnp.dot(input_rows, weight_pair, preferred_element_type=jnp.float32)
    gate = gate_up[:, :FF]
    upper = gate_up[:, FF:]
    sigma = jax.nn.sigmoid(gate)
    active = gate * sigma
    hidden = (active * upper).astype(jnp.bfloat16)
    output_rows = jnp.dot(hidden, weight_down, preferred_element_type=jnp.float32).astype(jnp.bfloat16)
    hidden_grad = jnp.dot(cot_rows, weight_down.T, preferred_element_type=jnp.float32)
    gate_cot = hidden_grad * upper * sigma * (1.0 + gate * (1.0 - sigma))
    upper_cot = hidden_grad * active
    pair_cot = jnp.concatenate([gate_cot, upper_cot], axis=1).astype(jnp.bfloat16)
    input_cot = jnp.dot(pair_cot, weight_pair.T, preferred_element_type=jnp.float32).astype(jnp.bfloat16)
    weight_cot = jnp.dot(input_rows.T, pair_cot, preferred_element_type=jnp.float32).astype(jnp.bfloat16)
    return output_rows, input_cot, weight_cot


def reference(tokens, cotangent, expert_ids, gate_probs, w_gate_up, w_down):
    group_rows = TOK_DEV * EXPERTS
    outputs = []
    in_grads = []
    prob_grads = []
    grad_total = jnp.zeros((EXPERTS, D, 2 * FF), jnp.float32)
    for replica in range(REPLICAS):
        start_row = replica * group_rows
        block_tokens = tokens[start_row:start_row + group_rows].reshape(EXPERTS, TOK_DEV, D)
        block_cot = cotangent[start_row:start_row + group_rows].reshape(EXPERTS, TOK_DEV, D)
        routes = expert_ids[start_row:start_row + group_rows].reshape(EXPERTS, TOK_DEV * TOP).astype(jnp.int32)
        weights = gate_probs[start_row:start_row + group_rows].reshape(EXPERTS, TOK_DEV, TOP)
        slot_rank = place_slots(routes)
        target_rows = (jnp.arange(EXPERTS, dtype=jnp.int32)[:, None] * CAP + slot_rank).astype(jnp.int32)
        token_copies = jnp.broadcast_to(block_tokens[:, :, None, :], (EXPERTS, TOK_DEV, TOP, D)).reshape(EXPERTS, TOK_DEV * TOP, D)
        cot_copies = (weights[:, :, :, None] * block_cot[:, :, None, :].astype(jnp.float32)).astype(jnp.bfloat16)
        cot_copies = cot_copies.reshape(EXPERTS, TOK_DEV * TOP, D)
        token_buffer = jnp.zeros((EXPERTS, EXPERTS * CAP, D), jnp.bfloat16).at[routes, target_rows].set(token_copies)
        cot_buffer = jnp.zeros((EXPERTS, EXPERTS * CAP, D), jnp.bfloat16).at[routes, target_rows].set(cot_copies)
        output_buffer, input_buffer, weight_cot = lax.map(expert_pass, (token_buffer, cot_buffer, w_gate_up, w_down))
        grad_total = grad_total + weight_cot.astype(jnp.float32)
        slot_out = output_buffer[routes, target_rows].reshape(EXPERTS, TOK_DEV, TOP, D)
        slot_in = input_buffer[routes, target_rows].reshape(EXPERTS, TOK_DEV, TOP, D)
        mixed = jnp.sum(weights[:, :, :, None] * slot_out.astype(jnp.float32), axis=2).astype(jnp.bfloat16)
        summed = jnp.sum(slot_in.astype(jnp.float32), axis=2).astype(jnp.bfloat16)
        inner = jnp.sum(block_cot[:, :, None, :].astype(jnp.float32) * slot_out.astype(jnp.float32), axis=3)
        outputs.append(mixed.reshape(group_rows, D))
        in_grads.append(summed.reshape(group_rows, D))
        prob_grads.append(inner.reshape(group_rows, TOP))
    layer_out = jnp.concatenate(outputs, axis=0)
    input_grad = jnp.concatenate(in_grads, axis=0)
    prob_grad = jnp.concatenate(prob_grads, axis=0)
    return layer_out, input_grad, prob_grad, grad_total.astype(jnp.bfloat16)
```

```python
import jax
import jax.numpy as jnp
from jax import lax
from jax.sharding import PartitionSpec as P


def gather_rows(own, axis_name, width):
    count = lax.axis_size(axis_name)
    me = lax.axis_index(axis_name)
    pieces = [(me, own)]
    for shift in range(1, count):
        moved = lax.ppermute(own, axis_name, [(i, (i + shift) % count) for i in range(count)])
        pieces.append(((me - shift) % count, moved))
    return pieces


def local(tokens, cotangent, expert_ids, gate_probs, w_gate_up, w_down):
    experts = lax.axis_size("expert")
    replicas = lax.axis_size("dp")
    me_dp = lax.axis_index("dp")
    token_count = tokens.shape[0]
    model_width = tokens.shape[1]
    top_count = expert_ids.shape[1]
    hidden_units = w_down.shape[1]
    block_rows = w_gate_up.shape[1]
    capacity = 4 * token_count * top_count // (3 * experts)
    weight_blocks = gather_rows(w_gate_up[0], "dp", block_rows)
    flat_routes = expert_ids.reshape(token_count * top_count)
    onehot = (flat_routes[:, None] == jnp.arange(experts, dtype=jnp.int32)[None, :]).astype(
        jnp.int32
    )
    before = jnp.cumsum(onehot, axis=0) - onehot
    slot_rank = jnp.sum(before * onehot, axis=1)
    target_rows = flat_routes * capacity + slot_rank
    token_copies = jnp.broadcast_to(tokens[:, None, :], (token_count, top_count, model_width))
    token_copies = token_copies.reshape(token_count * top_count, model_width)
    cot_copies = (gate_probs[:, :, None] * cotangent[:, None, :].astype(jnp.float32)).astype(
        jnp.bfloat16
    )
    cot_copies = cot_copies.reshape(token_count * top_count, model_width)
    both_copies = jnp.concatenate([token_copies, cot_copies], axis=1)
    both_send = (
        jnp.zeros((experts * capacity, 2 * model_width), jnp.bfloat16)
        .at[target_rows]
        .set(both_copies)
    )
    both_recv = lax.all_to_all(
        both_send.reshape(experts, capacity, 2 * model_width),
        "expert",
        split_axis=0,
        concat_axis=0,
        tiled=True,
    ).reshape(experts * capacity, 2 * model_width)
    input_rows = both_recv[:, :model_width]
    cot_rows = both_recv[:, model_width:]
    weight_down = w_down[0]

    def cols(block):
        return lax.dynamic_slice_in_dim(input_rows, block * block_rows, block_rows, axis=1)

    gate_up = None
    for block, weight in weight_blocks:
        part = jnp.dot(cols(block), weight, preferred_element_type=jnp.float32)
        gate_up = part if gate_up is None else gate_up + part
    gate = gate_up[:, :hidden_units]
    upper = gate_up[:, hidden_units:]
    sigma = jax.nn.sigmoid(gate)
    active = gate * sigma
    hidden = (active * upper).astype(jnp.bfloat16)
    output_rows = jnp.dot(hidden, weight_down, preferred_element_type=jnp.float32).astype(
        jnp.bfloat16
    )
    hidden_grad = lax.dot_general(
        cot_rows, weight_down, (((1,), (1,)), ((), ())), preferred_element_type=jnp.float32
    )
    gate_cot = hidden_grad * upper * sigma * (1.0 + gate * (1.0 - sigma))
    upper_cot = hidden_grad * active
    pair_cot = jnp.concatenate([gate_cot, upper_cot], axis=1).astype(jnp.bfloat16)
    input_cot = jnp.zeros((experts * capacity, model_width), jnp.bfloat16)
    for block, weight in weight_blocks:
        part = lax.dot_general(
            pair_cot, weight, (((1,), (1,)), ((), ())), preferred_element_type=jnp.float32
        ).astype(jnp.bfloat16)
        input_cot = lax.dynamic_update_slice_in_dim(input_cot, part, block * block_rows, axis=1)
    back = lax.all_to_all(
        jnp.concatenate([output_rows, input_cot], axis=1).reshape(
            experts, capacity, 2 * model_width
        ),
        "expert",
        split_axis=0,
        concat_axis=0,
        tiled=True,
    ).reshape(experts * capacity, 2 * model_width)
    slot_both = back[target_rows].reshape(token_count, top_count, 2 * model_width)
    slot_out = slot_both[:, :, :model_width]
    slot_in = slot_both[:, :, model_width:]
    layer_out = jnp.sum(gate_probs[:, :, None] * slot_out.astype(jnp.float32), axis=1).astype(
        jnp.bfloat16
    )
    input_grad = jnp.sum(slot_in.astype(jnp.float32), axis=1).astype(jnp.bfloat16)
    prob_grad = jnp.einsum("td,tkd->tk", cotangent, slot_out, preferred_element_type=jnp.float32)
    grad_rows = None
    for shift in range(replicas):
        block = (me_dp + shift) % replicas
        partial = lax.dot_general(
            cols(block), pair_cot, (((0,), (0,)), ((), ())), preferred_element_type=jnp.float32
        ).astype(jnp.bfloat16)
        if shift:
            partial = lax.ppermute(
                partial, "dp", [(i, (i + shift) % replicas) for i in range(replicas)]
            )
        grad_rows = (
            partial.astype(jnp.float32)
            if grad_rows is None
            else grad_rows + partial.astype(jnp.float32)
        )
    return (layer_out, input_grad, prob_grad, grad_rows.astype(jnp.bfloat16)[None])


def solution(mesh):
    placed = (
        P(("dp", "expert"), None),
        P(("dp", "expert"), None),
        P(("dp", "expert"), None),
        P(("dp", "expert"), None),
        P("expert", "dp", None),
        P("expert", None, None),
    )
    return jax.shard_map(
        local,
        mesh=mesh,
        in_specs=placed,
        out_specs=(
            P(("dp", "expert"), None),
            P(("dp", "expert"), None),
            P(("dp", "expert"), None),
            P("expert", "dp", None),
        ),
        check_vma=False,
    )
```

```python
import jax
import jax.numpy as jnp
from jax import lax
from jax.sharding import PartitionSpec as P


def gather_rows(own, axis_name, width):
    count = lax.axis_size(axis_name)
    me = lax.axis_index(axis_name)
    pieces = [(me, own)]
    for shift in range(1, count):
        moved = lax.ppermute(own, axis_name, [(i, (i + shift) % count) for i in range(count)])
        pieces.append(((me - shift) % count, moved))
    return pieces


def local(tokens, cotangent, expert_ids, gate_probs, w_gate_up, w_down):
    experts = lax.axis_size("expert")
    replicas = lax.axis_size("dp")
    me_dp = lax.axis_index("dp")
    token_count = tokens.shape[0]
    model_width = tokens.shape[1]
    top_count = expert_ids.shape[1]
    hidden_units = w_down.shape[1]
    block_rows = w_gate_up.shape[1]
    capacity = 4 * token_count * top_count // (3 * experts)
    weight_blocks = gather_rows(w_gate_up[0], "dp", block_rows)
    flat_routes = expert_ids.reshape(token_count * top_count)
    onehot = (flat_routes[:, None] == jnp.arange(experts, dtype=jnp.int32)[None, :]).astype(
        jnp.int32
    )
    before = jnp.cumsum(onehot, axis=0) - onehot
    slot_rank = jnp.sum(before * onehot, axis=1)
    target_rows = flat_routes * capacity + slot_rank
    slots = jnp.arange(experts * capacity, dtype=jnp.int32)
    chosen = target_rows.reshape(token_count, top_count)[None, :, :] == slots[:, None, None]
    pick = jnp.any(chosen, axis=2).astype(jnp.bfloat16)
    slot_prob = jnp.sum(jnp.where(chosen, gate_probs[None, :, :], 0.0), axis=(1, 2))
    token_send = jnp.dot(pick, tokens, preferred_element_type=jnp.float32).astype(jnp.bfloat16)
    cot_pick = jnp.dot(pick, cotangent, preferred_element_type=jnp.float32)
    cot_send = (slot_prob[:, None] * cot_pick).astype(jnp.bfloat16)
    both_send = jnp.concatenate([token_send, cot_send], axis=1)
    both_recv = lax.all_to_all(
        both_send.reshape(experts, capacity, 2 * model_width),
        "expert",
        split_axis=0,
        concat_axis=0,
        tiled=True,
    ).reshape(experts * capacity, 2 * model_width)
    input_rows = both_recv[:, :model_width]
    cot_rows = both_recv[:, model_width:]
    weight_down = w_down[0]

    def cols(block):
        return lax.dynamic_slice_in_dim(input_rows, block * block_rows, block_rows, axis=1)

    gate_up = None
    for block, weight in weight_blocks:
        part = jnp.dot(cols(block), weight, preferred_element_type=jnp.float32)
        gate_up = part if gate_up is None else gate_up + part
    gate = gate_up[:, :hidden_units]
    upper = gate_up[:, hidden_units:]
    sigma = jax.nn.sigmoid(gate)
    active = gate * sigma
    hidden = (active * upper).astype(jnp.bfloat16)
    output_rows = jnp.dot(hidden, weight_down, preferred_element_type=jnp.float32).astype(
        jnp.bfloat16
    )
    hidden_grad = lax.dot_general(
        cot_rows, weight_down, (((1,), (1,)), ((), ())), preferred_element_type=jnp.float32
    )
    gate_cot = hidden_grad * upper * sigma * (1.0 + gate * (1.0 - sigma))
    upper_cot = hidden_grad * active
    pair_cot = jnp.concatenate([gate_cot, upper_cot], axis=1).astype(jnp.bfloat16)
    input_cot = jnp.zeros((experts * capacity, model_width), jnp.bfloat16)
    for block, weight in weight_blocks:
        part = lax.dot_general(
            pair_cot, weight, (((1,), (1,)), ((), ())), preferred_element_type=jnp.float32
        ).astype(jnp.bfloat16)
        input_cot = lax.dynamic_update_slice_in_dim(input_cot, part, block * block_rows, axis=1)
    back = lax.all_to_all(
        jnp.concatenate([output_rows, input_cot], axis=1).reshape(
            experts, capacity, 2 * model_width
        ),
        "expert",
        split_axis=0,
        concat_axis=0,
        tiled=True,
    ).reshape(experts * capacity, 2 * model_width)
    back_out = back[:, :model_width]
    back_in = back[:, model_width:]
    owned = target_rows.reshape(token_count, top_count)[:, :, None] == slots[None, None, :]
    weights = jnp.sum(jnp.where(owned, gate_probs[:, :, None], 0.0), axis=1)
    layer_out = jnp.dot(
        weights,
        back_out.astype(jnp.float32),
        precision=lax.Precision.HIGHEST,
        preferred_element_type=jnp.float32,
    ).astype(jnp.bfloat16)
    gathered = jnp.any(owned, axis=1).astype(jnp.bfloat16)
    input_grad = jnp.dot(gathered, back_in, preferred_element_type=jnp.float32).astype(
        jnp.bfloat16
    )
    inner = lax.dot_general(
        cotangent, back_out, (((1,), (1,)), ((), ())), preferred_element_type=jnp.float32
    )
    prob_grad = jnp.sum(jnp.where(owned, inner[:, None, :], 0.0), axis=2)
    grad_rows = None
    for shift in range(replicas):
        block = (me_dp + shift) % replicas
        partial = lax.dot_general(
            cols(block), pair_cot, (((0,), (0,)), ((), ())), preferred_element_type=jnp.float32
        ).astype(jnp.bfloat16)
        if shift:
            partial = lax.ppermute(
                partial, "dp", [(i, (i + shift) % replicas) for i in range(replicas)]
            )
        grad_rows = (
            partial.astype(jnp.float32)
            if grad_rows is None
            else grad_rows + partial.astype(jnp.float32)
        )
    return (layer_out, input_grad, prob_grad, grad_rows.astype(jnp.bfloat16)[None])


def solution(mesh):
    placed = (
        P(("dp", "expert"), None),
        P(("dp", "expert"), None),
        P(("dp", "expert"), None),
        P(("dp", "expert"), None),
        P("expert", "dp", None),
        P("expert", None, None),
    )
    return jax.shard_map(
        local,
        mesh=mesh,
        in_specs=placed,
        out_specs=(
            P(("dp", "expert"), None),
            P(("dp", "expert"), None),
            P(("dp", "expert"), None),
            P("expert", "dp", None),
        ),
        check_vma=False,
    )
```

```python
import jax
import jax.numpy as jnp
from jax import lax
from jax.sharding import PartitionSpec as P

CHUNKS = 2


def gather_rows(own, axis_name):
    count = lax.axis_size(axis_name)
    me = lax.axis_index(axis_name)
    pieces = [(me, own)]
    for shift in range(1, count):
        moved = lax.ppermute(own, axis_name, [(i, (i + shift) % count) for i in range(count)])
        pieces.append(((me - shift) % count, moved))
    return pieces


def local(tokens, cotangent, expert_ids, gate_probs, w_gate_up, w_down):
    experts = lax.axis_size("expert")
    replicas = lax.axis_size("dp")
    me_dp = lax.axis_index("dp")
    token_count = tokens.shape[0]
    model_width = tokens.shape[1]
    top_count = expert_ids.shape[1]
    hidden_units = w_down.shape[1]
    block_rows = w_gate_up.shape[1]
    capacity = 4 * token_count * top_count // (3 * experts)
    chunks = CHUNKS if capacity % CHUNKS == 0 else 1
    part_cap = capacity // chunks
    weight_blocks = gather_rows(w_gate_up[0], "dp")
    weight_down = w_down[0]
    flat_routes = expert_ids.reshape(token_count * top_count)
    onehot = (flat_routes[:, None] == jnp.arange(experts, dtype=jnp.int32)[None, :]).astype(
        jnp.int32
    )
    before = jnp.cumsum(onehot, axis=0) - onehot
    slot_rank = jnp.sum(before * onehot, axis=1)
    target_rows = (flat_routes * capacity + slot_rank).reshape(token_count, top_count)
    slots = jnp.arange(experts * capacity, dtype=jnp.int32)
    chosen = target_rows[None, :, :] == slots[:, None, None]
    pick = jnp.any(chosen, axis=2).astype(jnp.bfloat16)
    slot_prob = jnp.sum(jnp.where(chosen, gate_probs[None, :, :], 0.0), axis=(1, 2))
    picked = jnp.dot(
        pick, jnp.concatenate([tokens, cotangent], axis=1), preferred_element_type=jnp.float32
    )
    both_send = jnp.concatenate(
        [picked[:, :model_width], slot_prob[:, None] * picked[:, model_width:]], axis=1
    ).astype(jnp.bfloat16)
    both_send = both_send.reshape(experts, capacity, 2 * model_width)

    def exchange(block):
        return lax.all_to_all(block, "expert", split_axis=0, concat_axis=0, tiled=True)

    def cols(rows, block):
        return lax.dynamic_slice_in_dim(rows, block * block_rows, block_rows, axis=1)

    received = [
        exchange(both_send[:, c * part_cap : (c + 1) * part_cap]).reshape(
            experts * part_cap, 2 * model_width
        )
        for c in range(chunks)
    ]
    returned = []
    grads = [None] * replicas
    for recv in received:
        input_rows = recv[:, :model_width]
        cot_rows = recv[:, model_width:]
        gate_up = None
        for block, weight in weight_blocks:
            part = jnp.dot(cols(input_rows, block), weight, preferred_element_type=jnp.float32)
            gate_up = part if gate_up is None else gate_up + part
        gate = gate_up[:, :hidden_units]
        upper = gate_up[:, hidden_units:]
        sigma = jax.nn.sigmoid(gate)
        active = gate * sigma
        hidden = (active * upper).astype(jnp.bfloat16)
        output_rows = jnp.dot(hidden, weight_down, preferred_element_type=jnp.float32).astype(
            jnp.bfloat16
        )
        hidden_grad = lax.dot_general(
            cot_rows, weight_down, (((1,), (1,)), ((), ())), preferred_element_type=jnp.float32
        )
        gate_cot = hidden_grad * upper * sigma * (1.0 + gate * (1.0 - sigma))
        upper_cot = hidden_grad * active
        pair_cot = jnp.concatenate([gate_cot, upper_cot], axis=1).astype(jnp.bfloat16)
        input_cot = jnp.zeros((experts * part_cap, model_width), jnp.bfloat16)
        for block, weight in weight_blocks:
            part = lax.dot_general(
                pair_cot, weight, (((1,), (1,)), ((), ())), preferred_element_type=jnp.float32
            ).astype(jnp.bfloat16)
            input_cot = lax.dynamic_update_slice_in_dim(
                input_cot, part, block * block_rows, axis=1
            )
        back = exchange(
            jnp.concatenate([output_rows, input_cot], axis=1).reshape(
                experts, part_cap, 2 * model_width
            )
        )
        returned.append(back)
        for shift in range(replicas):
            block = (me_dp + shift) % replicas
            partial = lax.dot_general(
                cols(input_rows, block),
                pair_cot,
                (((0,), (0,)), ((), ())),
                preferred_element_type=jnp.float32,
            )
            grads[shift] = partial if grads[shift] is None else grads[shift] + partial
    grad_rows = lax.optimization_barrier(grads[0])
    for shift in range(1, replicas):
        moved = lax.ppermute(
            grads[shift].astype(jnp.bfloat16),
            "dp",
            [(i, (i + shift) % replicas) for i in range(replicas)],
        )
        grad_rows = grad_rows + moved.astype(jnp.float32)
    back = jnp.concatenate(returned, axis=1).reshape(experts * capacity, 2 * model_width)
    back_out = back[:, :model_width]
    back_in = back[:, model_width:]
    owned = target_rows[:, :, None] == slots[None, None, :]
    weights = jnp.sum(jnp.where(owned, gate_probs[:, :, None], 0.0), axis=1)
    layer_out = jnp.dot(
        weights,
        back_out.astype(jnp.float32),
        precision=lax.Precision.HIGHEST,
        preferred_element_type=jnp.float32,
    ).astype(jnp.bfloat16)
    gathered = jnp.any(owned, axis=1).astype(jnp.bfloat16)
    input_grad = jnp.dot(gathered, back_in, preferred_element_type=jnp.float32).astype(
        jnp.bfloat16
    )
    inner = lax.dot_general(
        cotangent, back_out, (((1,), (1,)), ((), ())), preferred_element_type=jnp.float32
    )
    prob_grad = jnp.sum(jnp.where(owned, inner[:, None, :], 0.0), axis=2)
    return (layer_out, input_grad, prob_grad, grad_rows.astype(jnp.bfloat16)[None])


def solution(mesh):
    placed = (
        P(("dp", "expert"), None),
        P(("dp", "expert"), None),
        P(("dp", "expert"), None),
        P(("dp", "expert"), None),
        P("expert", "dp", None),
        P("expert", None, None),
    )
    return jax.shard_map(
        local,
        mesh=mesh,
        in_specs=placed,
        out_specs=(
            P(("dp", "expert"), None),
            P(("dp", "expert"), None),
            P(("dp", "expert"), None),
            P("expert", "dp", None),
        ),
        check_vma=False,
    )
```

```python
import jax
import jax.numpy as jnp
from jax import lax
from jax.sharding import PartitionSpec as P


def gather_rows(own, axis_name, width):
    count = lax.axis_size(axis_name)
    me = lax.axis_index(axis_name)
    pieces = [(me, own)]
    for shift in range(1, count):
        moved = lax.ppermute(own, axis_name, [(i, (i + shift) % count) for i in range(count)])
        pieces.append(((me - shift) % count, moved))
    return pieces


def local(tokens, cotangent, expert_ids, gate_probs, w_gate_up, w_down):
    experts = lax.axis_size("expert")
    replicas = lax.axis_size("dp")
    me_dp = lax.axis_index("dp")
    token_count = tokens.shape[0]
    model_width = tokens.shape[1]
    top_count = expert_ids.shape[1]
    hidden_units = w_down.shape[1]
    block_rows = w_gate_up.shape[1]
    capacity = 4 * token_count * top_count // (3 * experts)
    weight_blocks = gather_rows(w_gate_up[0], "dp", block_rows)
    stacked = jnp.stack([weight for _, weight in weight_blocks])
    order = (me_dp - jnp.arange(replicas, dtype=jnp.int32)) % replicas
    weight_fwd = jnp.take(stacked, order, axis=0).reshape(replicas * block_rows, -1)
    flat_routes = expert_ids.reshape(token_count * top_count)
    onehot = (flat_routes[:, None] == jnp.arange(experts, dtype=jnp.int32)[None, :]).astype(
        jnp.int32
    )
    before = jnp.cumsum(onehot, axis=0) - onehot
    slot_rank = jnp.sum(before * onehot, axis=1)
    target_rows = flat_routes * capacity + slot_rank
    slots = jnp.arange(experts * capacity, dtype=jnp.int32)
    chosen = target_rows.reshape(token_count, top_count)[None, :, :] == slots[:, None, None]
    pick = jnp.any(chosen, axis=2).astype(jnp.bfloat16)
    slot_prob = jnp.sum(jnp.where(chosen, gate_probs[None, :, :], 0.0), axis=(1, 2))
    token_send = jnp.dot(pick, tokens, preferred_element_type=jnp.float32).astype(jnp.bfloat16)
    cot_pick = jnp.dot(pick, cotangent, preferred_element_type=jnp.float32)
    cot_send = (slot_prob[:, None] * cot_pick).astype(jnp.bfloat16)
    both_send = jnp.concatenate([token_send, cot_send], axis=1)
    both_recv = lax.all_to_all(
        both_send.reshape(experts, capacity, 2 * model_width),
        "expert",
        split_axis=0,
        concat_axis=0,
        tiled=True,
    ).reshape(experts * capacity, 2 * model_width)
    input_rows = both_recv[:, :model_width]
    cot_rows = both_recv[:, model_width:]
    weight_down = w_down[0]

    gate_up = jnp.dot(input_rows, weight_fwd, preferred_element_type=jnp.float32)
    gate = gate_up[:, :hidden_units]
    upper = gate_up[:, hidden_units:]
    sigma = jax.nn.sigmoid(gate)
    active = gate * sigma
    hidden = (active * upper).astype(jnp.bfloat16)
    output_rows = jnp.dot(hidden, weight_down, preferred_element_type=jnp.float32).astype(
        jnp.bfloat16
    )
    hidden_grad = lax.dot_general(
        cot_rows, weight_down, (((1,), (1,)), ((), ())), preferred_element_type=jnp.float32
    )
    gate_cot = hidden_grad * upper * sigma * (1.0 + gate * (1.0 - sigma))
    upper_cot = hidden_grad * active
    pair_cot = jnp.concatenate([gate_cot, upper_cot], axis=1).astype(jnp.bfloat16)
    input_cot = lax.dot_general(
        pair_cot, weight_fwd, (((1,), (1,)), ((), ())), preferred_element_type=jnp.float32
    ).astype(jnp.bfloat16)
    back = lax.all_to_all(
        jnp.concatenate([output_rows, input_cot], axis=1).reshape(
            experts, capacity, 2 * model_width
        ),
        "expert",
        split_axis=0,
        concat_axis=0,
        tiled=True,
    ).reshape(experts * capacity, 2 * model_width)
    owned = (target_rows.reshape(token_count * top_count)[:, None] == slots[None, :]).astype(
        jnp.bfloat16
    )
    slot_both = jnp.dot(owned, back, preferred_element_type=jnp.float32).reshape(
        token_count, top_count, 2 * model_width
    )
    slot_out = slot_both[:, :, :model_width]
    slot_in = slot_both[:, :, model_width:]
    layer_out = jnp.sum(gate_probs[:, :, None] * slot_out, axis=1).astype(jnp.bfloat16)
    input_grad = jnp.sum(slot_in, axis=1).astype(jnp.bfloat16)
    prob_grad = jnp.sum(cotangent[:, None, :].astype(jnp.float32) * slot_out, axis=2)
    weight_cot = lax.dot_general(
        input_rows, pair_cot, (((0,), (0,)), ((), ())), preferred_element_type=jnp.float32
    )

    def grad_block(block):
        return lax.dynamic_slice_in_dim(weight_cot, block * block_rows, block_rows, axis=0)

    grad_rows = grad_block(me_dp)
    for shift in range(1, replicas):
        moved = lax.ppermute(
            grad_block((me_dp + shift) % replicas).astype(jnp.bfloat16),
            "dp",
            [(i, (i + shift) % replicas) for i in range(replicas)],
        )
        grad_rows = grad_rows + moved.astype(jnp.float32)
    return (layer_out, input_grad, prob_grad, grad_rows.astype(jnp.bfloat16)[None])


def solution(mesh):
    placed = (
        P(("dp", "expert"), None),
        P(("dp", "expert"), None),
        P(("dp", "expert"), None),
        P(("dp", "expert"), None),
        P("expert", "dp", None),
        P("expert", None, None),
    )
    return jax.shard_map(
        local,
        mesh=mesh,
        in_specs=placed,
        out_specs=(
            P(("dp", "expert"), None),
            P(("dp", "expert"), None),
            P(("dp", "expert"), None),
            P("expert", "dp", None),
        ),
        check_vma=False,
    )
```

```python
import jax
import jax.numpy as jnp
from jax import lax
from jax.sharding import PartitionSpec as P


def gather_rows(own, axis_name, width):
    count = lax.axis_size(axis_name)
    me = lax.axis_index(axis_name)
    pieces = [(me, own)]
    for shift in range(1, count):
        moved = lax.ppermute(own, axis_name, [(i, (i + shift) % count) for i in range(count)])
        pieces.append(((me - shift) % count, moved))
    return pieces


def local(tokens, cotangent, expert_ids, gate_probs, w_gate_up, w_down):
    experts = lax.axis_size("expert")
    replicas = lax.axis_size("dp")
    me_dp = lax.axis_index("dp")
    token_count = tokens.shape[0]
    model_width = tokens.shape[1]
    top_count = expert_ids.shape[1]
    hidden_units = w_down.shape[1]
    block_rows = w_gate_up.shape[1]
    capacity = 4 * token_count * top_count // (3 * experts)
    weight_blocks = gather_rows(w_gate_up[0], "dp", block_rows)
    flat_routes = expert_ids.reshape(token_count * top_count)
    onehot = (flat_routes[:, None] == jnp.arange(experts, dtype=jnp.int32)[None, :]).astype(
        jnp.int32
    )
    before = jnp.cumsum(onehot, axis=0) - onehot
    slot_rank = jnp.sum(before * onehot, axis=1)
    target_rows = flat_routes * capacity + slot_rank
    slots = jnp.arange(experts * capacity, dtype=jnp.int32)
    chosen = target_rows.reshape(token_count, top_count)[None, :, :] == slots[:, None, None]
    pick = jnp.any(chosen, axis=2).astype(jnp.bfloat16)
    slot_prob = jnp.sum(jnp.where(chosen, gate_probs[None, :, :], 0.0), axis=(1, 2))
    token_send = jnp.dot(pick, tokens, preferred_element_type=jnp.float32).astype(jnp.bfloat16)
    cot_pick = jnp.dot(pick, cotangent, preferred_element_type=jnp.float32)
    cot_send = (slot_prob[:, None] * cot_pick).astype(jnp.bfloat16)
    both_send = jnp.concatenate([token_send, cot_send], axis=1)
    both_recv = lax.all_to_all(
        both_send.reshape(experts, capacity, 2 * model_width),
        "expert",
        split_axis=0,
        concat_axis=0,
        tiled=True,
    ).reshape(experts * capacity, 2 * model_width)
    input_rows = both_recv[:, :model_width]
    cot_rows = both_recv[:, model_width:]
    weight_down = w_down[0]


    def cols(block):
        return lax.dynamic_slice_in_dim(input_rows, block * block_rows, block_rows, axis=1)

    gate_up = None
    for block, weight in weight_blocks:
        part = jnp.dot(cols(block), weight, preferred_element_type=jnp.float32)
        gate_up = part if gate_up is None else gate_up + part
    gate = gate_up[:, :hidden_units]
    upper = gate_up[:, hidden_units:]
    sigma = jax.nn.sigmoid(gate)
    active = gate * sigma
    hidden = (active * upper).astype(jnp.bfloat16)
    output_rows = jnp.dot(hidden, weight_down, preferred_element_type=jnp.float32).astype(
        jnp.bfloat16
    )
    hidden_grad = lax.dot_general(
        cot_rows, weight_down, (((1,), (1,)), ((), ())), preferred_element_type=jnp.float32
    )
    gate_cot = hidden_grad * upper * sigma * (1.0 + gate * (1.0 - sigma))
    upper_cot = hidden_grad * active
    pair_cot = jnp.concatenate([gate_cot, upper_cot], axis=1).astype(jnp.bfloat16)
    input_cot = jnp.zeros((experts * capacity, model_width), jnp.bfloat16)
    for block, weight in weight_blocks:
        part = lax.dot_general(
            pair_cot, weight, (((1,), (1,)), ((), ())), preferred_element_type=jnp.float32
        ).astype(jnp.bfloat16)
        input_cot = lax.dynamic_update_slice_in_dim(input_cot, part, block * block_rows, axis=1)
    back = lax.all_to_all(
        jnp.concatenate([output_rows, input_cot], axis=1).reshape(
            experts, capacity, 2 * model_width
        ),
        "expert",
        split_axis=0,
        concat_axis=0,
        tiled=True,
    ).reshape(experts * capacity, 2 * model_width)
    owned = (target_rows.reshape(token_count * top_count)[:, None] == slots[None, :]).astype(
        jnp.bfloat16
    )
    slot_both = jnp.dot(owned, back, preferred_element_type=jnp.float32).reshape(
        token_count, top_count, 2 * model_width
    )
    slot_out = slot_both[:, :, :model_width]
    slot_in = slot_both[:, :, model_width:]
    layer_out = jnp.sum(gate_probs[:, :, None] * slot_out, axis=1).astype(jnp.bfloat16)
    input_grad = jnp.sum(slot_in, axis=1).astype(jnp.bfloat16)
    prob_grad = jnp.sum(cotangent[:, None, :].astype(jnp.float32) * slot_out, axis=2)
    weight_cot = lax.dot_general(
        input_rows, pair_cot, (((0,), (0,)), ((), ())), preferred_element_type=jnp.float32
    )

    def grad_block(block):
        return lax.dynamic_slice_in_dim(weight_cot, block * block_rows, block_rows, axis=0)

    grad_rows = grad_block(me_dp)
    for shift in range(1, replicas):
        moved = lax.ppermute(
            grad_block((me_dp + shift) % replicas).astype(jnp.bfloat16),
            "dp",
            [(i, (i + shift) % replicas) for i in range(replicas)],
        )
        grad_rows = grad_rows + moved.astype(jnp.float32)
    return (layer_out, input_grad, prob_grad, grad_rows.astype(jnp.bfloat16)[None])


def solution(mesh):
    placed = (
        P(("dp", "expert"), None),
        P(("dp", "expert"), None),
        P(("dp", "expert"), None),
        P(("dp", "expert"), None),
        P("expert", "dp", None),
        P("expert", None, None),
    )
    return jax.shard_map(
        local,
        mesh=mesh,
        in_specs=placed,
        out_specs=(
            P(("dp", "expert"), None),
            P(("dp", "expert"), None),
            P(("dp", "expert"), None),
            P("expert", "dp", None),
        ),
        check_vma=False,
    )
```

```python
import jax
import jax.numpy as jnp
from jax import lax
from jax.sharding import PartitionSpec as P


def gather_rows(own, axis_name, width):
    count = lax.axis_size(axis_name)
    me = lax.axis_index(axis_name)
    pieces = [(me, own)]
    for shift in range(1, count):
        moved = lax.ppermute(own, axis_name, [(i, (i + shift) % count) for i in range(count)])
        pieces.append(((me - shift) % count, moved))
    return pieces


def local(tokens, cotangent, expert_ids, gate_probs, w_gate_up, w_down):
    experts = lax.axis_size("expert")
    replicas = lax.axis_size("dp")
    me_dp = lax.axis_index("dp")
    token_count = tokens.shape[0]
    model_width = tokens.shape[1]
    top_count = expert_ids.shape[1]
    hidden_units = w_down.shape[1]
    block_rows = w_gate_up.shape[1]
    capacity = 4 * token_count * top_count // (3 * experts)
    weight_blocks = gather_rows(w_gate_up[0], "dp", block_rows)
    flat_routes = expert_ids.reshape(token_count * top_count)
    onehot = (flat_routes[:, None] == jnp.arange(experts, dtype=jnp.int32)[None, :]).astype(
        jnp.int32
    )
    before = jnp.cumsum(onehot, axis=0) - onehot
    slot_rank = jnp.sum(before * onehot, axis=1)
    target_rows = flat_routes * capacity + slot_rank
    slots = jnp.arange(experts * capacity, dtype=jnp.int32)
    chosen = target_rows.reshape(token_count, top_count)[None, :, :] == slots[:, None, None]
    pick = jnp.any(chosen, axis=2).astype(jnp.bfloat16)
    slot_prob = jnp.sum(jnp.where(chosen, gate_probs[None, :, :], 0.0), axis=(1, 2))
    token_send = jnp.dot(pick, tokens, preferred_element_type=jnp.float32).astype(jnp.bfloat16)
    cot_pick = jnp.dot(pick, cotangent, preferred_element_type=jnp.float32)
    cot_send = (slot_prob[:, None] * cot_pick).astype(jnp.bfloat16)
    both_send = jnp.zeros((experts * capacity, 2 * model_width), jnp.bfloat16)
    both_send = lax.dynamic_update_slice_in_dim(both_send, token_send, 0, axis=1)
    both_send = lax.dynamic_update_slice_in_dim(both_send, cot_send, model_width, axis=1)
    both_recv = lax.all_to_all(
        both_send.reshape(experts, capacity, 2 * model_width),
        "expert",
        split_axis=0,
        concat_axis=0,
        tiled=True,
    ).reshape(experts * capacity, 2 * model_width)
    input_rows = both_recv[:, :model_width]
    cot_rows = both_recv[:, model_width:]
    weight_down = w_down[0]


    def cols(block):
        return lax.dynamic_slice_in_dim(input_rows, block * block_rows, block_rows, axis=1)

    gate_up = None
    for block, weight in weight_blocks:
        part = jnp.dot(cols(block), weight, preferred_element_type=jnp.float32)
        gate_up = part if gate_up is None else gate_up + part
    gate = gate_up[:, :hidden_units]
    upper = gate_up[:, hidden_units:]
    sigma = jax.nn.sigmoid(gate)
    active = gate * sigma
    hidden = (active * upper).astype(jnp.bfloat16)
    output_rows = jnp.dot(hidden, weight_down, preferred_element_type=jnp.float32).astype(
        jnp.bfloat16
    )
    hidden_grad = lax.dot_general(
        cot_rows, weight_down, (((1,), (1,)), ((), ())), preferred_element_type=jnp.float32
    )
    gate_cot = hidden_grad * upper * sigma * (1.0 + gate * (1.0 - sigma))
    upper_cot = hidden_grad * active
    pair_cot = jnp.concatenate([gate_cot, upper_cot], axis=1).astype(jnp.bfloat16)
    send_back = jnp.zeros((experts * capacity, 2 * model_width), jnp.bfloat16)
    send_back = lax.dynamic_update_slice_in_dim(send_back, output_rows, 0, axis=1)
    for block, weight in weight_blocks:
        part = lax.dot_general(
            pair_cot, weight, (((1,), (1,)), ((), ())), preferred_element_type=jnp.float32
        ).astype(jnp.bfloat16)
        send_back = lax.dynamic_update_slice_in_dim(
            send_back, part, model_width + block * block_rows, axis=1
        )
    back = lax.all_to_all(
        send_back.reshape(
            experts, capacity, 2 * model_width
        ),
        "expert",
        split_axis=0,
        concat_axis=0,
        tiled=True,
    ).reshape(experts * capacity, 2 * model_width)
    owned = (target_rows.reshape(token_count * top_count)[:, None] == slots[None, :]).astype(
        jnp.bfloat16
    )
    slot_both = jnp.dot(owned, back, preferred_element_type=jnp.float32).reshape(
        token_count, top_count, 2 * model_width
    )
    slot_out = slot_both[:, :, :model_width]
    slot_in = slot_both[:, :, model_width:]
    layer_out = jnp.sum(gate_probs[:, :, None] * slot_out, axis=1).astype(jnp.bfloat16)
    input_grad = jnp.sum(slot_in, axis=1).astype(jnp.bfloat16)
    prob_grad = jnp.sum(cotangent[:, None, :].astype(jnp.float32) * slot_out, axis=2)
    weight_cot = lax.dot_general(
        input_rows, pair_cot, (((0,), (0,)), ((), ())), preferred_element_type=jnp.float32
    )

    def grad_block(block):
        return lax.dynamic_slice_in_dim(weight_cot, block * block_rows, block_rows, axis=0)

    grad_rows = grad_block(me_dp)
    for shift in range(1, replicas):
        moved = lax.ppermute(
            grad_block((me_dp + shift) % replicas).astype(jnp.bfloat16),
            "dp",
            [(i, (i + shift) % replicas) for i in range(replicas)],
        )
        grad_rows = grad_rows + moved.astype(jnp.float32)
    return (layer_out, input_grad, prob_grad, grad_rows.astype(jnp.bfloat16)[None])


def solution(mesh):
    placed = (
        P(("dp", "expert"), None),
        P(("dp", "expert"), None),
        P(("dp", "expert"), None),
        P(("dp", "expert"), None),
        P("expert", "dp", None),
        P("expert", None, None),
    )
    return jax.shard_map(
        local,
        mesh=mesh,
        in_specs=placed,
        out_specs=(
            P(("dp", "expert"), None),
            P(("dp", "expert"), None),
            P(("dp", "expert"), None),
            P("expert", "dp", None),
        ),
        check_vma=False,
    )
```

```python
import jax
import jax.numpy as jnp
from jax import lax
from jax.sharding import PartitionSpec as P


def gather_rows(own, axis_name, width):
    count = lax.axis_size(axis_name)
    me = lax.axis_index(axis_name)
    pieces = [(me, own)]
    for shift in range(1, count):
        moved = lax.ppermute(own, axis_name, [(i, (i + shift) % count) for i in range(count)])
        pieces.append(((me - shift) % count, moved))
    return pieces


def local(tokens, cotangent, expert_ids, gate_probs, w_gate_up, w_down):
    experts = lax.axis_size("expert")
    replicas = lax.axis_size("dp")
    me_dp = lax.axis_index("dp")
    token_count = tokens.shape[0]
    model_width = tokens.shape[1]
    top_count = expert_ids.shape[1]
    hidden_units = w_down.shape[1]
    block_rows = w_gate_up.shape[1]
    capacity = 4 * token_count * top_count // (3 * experts)
    weight_blocks = gather_rows(w_gate_up[0], "dp", block_rows)
    flat_routes = expert_ids.reshape(token_count * top_count)
    onehot = (flat_routes[:, None] == jnp.arange(experts, dtype=jnp.int32)[None, :]).astype(
        jnp.int32
    )
    before = jnp.cumsum(onehot, axis=0) - onehot
    slot_rank = jnp.sum(before * onehot, axis=1)
    target_rows = flat_routes * capacity + slot_rank
    slots = jnp.arange(experts * capacity, dtype=jnp.int32)
    chosen = target_rows.reshape(token_count, top_count)[None, :, :] == slots[:, None, None]
    pick = jnp.any(chosen, axis=2).astype(jnp.bfloat16)
    slot_prob = jnp.sum(jnp.where(chosen, gate_probs[None, :, :], 0.0), axis=(1, 2))
    picked = jnp.dot(
        pick, jnp.concatenate([tokens, cotangent], axis=1), preferred_element_type=jnp.float32
    )
    columns = lax.broadcasted_iota(jnp.int32, picked.shape, 1)
    scale = jnp.where(columns < model_width, 1.0, slot_prob[:, None])
    both_send = (picked * scale).astype(jnp.bfloat16)
    both_recv = lax.all_to_all(
        both_send.reshape(experts, capacity, 2 * model_width),
        "expert",
        split_axis=0,
        concat_axis=0,
        tiled=True,
    ).reshape(experts * capacity, 2 * model_width)
    input_rows = both_recv[:, :model_width]
    cot_rows = both_recv[:, model_width:]
    weight_down = w_down[0]


    def cols(block):
        return lax.dynamic_slice_in_dim(input_rows, block * block_rows, block_rows, axis=1)

    gate_up = None
    for block, weight in weight_blocks:
        part = jnp.dot(cols(block), weight, preferred_element_type=jnp.float32)
        gate_up = part if gate_up is None else gate_up + part
    gate = gate_up[:, :hidden_units]
    upper = gate_up[:, hidden_units:]
    sigma = jax.nn.sigmoid(gate)
    active = gate * sigma
    hidden = (active * upper).astype(jnp.bfloat16)
    output_rows = jnp.dot(hidden, weight_down, preferred_element_type=jnp.float32).astype(
        jnp.bfloat16
    )
    hidden_grad = lax.dot_general(
        cot_rows, weight_down, (((1,), (1,)), ((), ())), preferred_element_type=jnp.float32
    )
    gate_cot = hidden_grad * upper * sigma * (1.0 + gate * (1.0 - sigma))
    upper_cot = hidden_grad * active
    pair_cot = jnp.concatenate([gate_cot, upper_cot], axis=1).astype(jnp.bfloat16)
    send_back = jnp.zeros((experts * capacity, 2 * model_width), jnp.bfloat16)
    send_back = lax.dynamic_update_slice_in_dim(send_back, output_rows, 0, axis=1)
    for block, weight in weight_blocks:
        part = lax.dot_general(
            pair_cot, weight, (((1,), (1,)), ((), ())), preferred_element_type=jnp.float32
        ).astype(jnp.bfloat16)
        send_back = lax.dynamic_update_slice_in_dim(
            send_back, part, model_width + block * block_rows, axis=1
        )
    back = lax.all_to_all(
        send_back.reshape(
            experts, capacity, 2 * model_width
        ),
        "expert",
        split_axis=0,
        concat_axis=0,
        tiled=True,
    ).reshape(experts * capacity, 2 * model_width)
    owned = (target_rows.reshape(token_count * top_count)[:, None] == slots[None, :]).astype(
        jnp.bfloat16
    )
    slot_both = jnp.dot(owned, back, preferred_element_type=jnp.float32).reshape(
        token_count, top_count, 2 * model_width
    )
    slot_out = slot_both[:, :, :model_width]
    slot_in = slot_both[:, :, model_width:]
    layer_out = jnp.sum(gate_probs[:, :, None] * slot_out, axis=1).astype(jnp.bfloat16)
    input_grad = jnp.sum(slot_in, axis=1).astype(jnp.bfloat16)
    prob_grad = jnp.sum(cotangent[:, None, :].astype(jnp.float32) * slot_out, axis=2)
    weight_cot = lax.dot_general(
        input_rows, pair_cot, (((0,), (0,)), ((), ())), preferred_element_type=jnp.float32
    )

    def grad_block(block):
        return lax.dynamic_slice_in_dim(weight_cot, block * block_rows, block_rows, axis=0)

    grad_rows = grad_block(me_dp)
    for shift in range(1, replicas):
        moved = lax.ppermute(
            grad_block((me_dp + shift) % replicas).astype(jnp.bfloat16),
            "dp",
            [(i, (i + shift) % replicas) for i in range(replicas)],
        )
        grad_rows = grad_rows + moved.astype(jnp.float32)
    return (layer_out, input_grad, prob_grad, grad_rows.astype(jnp.bfloat16)[None])


def solution(mesh):
    placed = (
        P(("dp", "expert"), None),
        P(("dp", "expert"), None),
        P(("dp", "expert"), None),
        P(("dp", "expert"), None),
        P("expert", "dp", None),
        P("expert", None, None),
    )
    return jax.shard_map(
        local,
        mesh=mesh,
        in_specs=placed,
        out_specs=(
            P(("dp", "expert"), None),
            P(("dp", "expert"), None),
            P(("dp", "expert"), None),
            P("expert", "dp", None),
        ),
        check_vma=False,
    )
```

```python
import jax
import jax.numpy as jnp
from jax import lax
from jax.sharding import PartitionSpec as P


def gather_rows(own, axis_name, width):
    count = lax.axis_size(axis_name)
    me = lax.axis_index(axis_name)
    pieces = [(me, own)]
    for shift in range(1, count):
        moved = lax.ppermute(own, axis_name, [(i, (i + shift) % count) for i in range(count)])
        pieces.append(((me - shift) % count, moved))
    return pieces


def local(tokens, cotangent, expert_ids, gate_probs, w_gate_up, w_down):
    experts = lax.axis_size("expert")
    replicas = lax.axis_size("dp")
    me_dp = lax.axis_index("dp")
    token_count = tokens.shape[0]
    model_width = tokens.shape[1]
    top_count = expert_ids.shape[1]
    hidden_units = w_down.shape[1]
    block_rows = w_gate_up.shape[1]
    capacity = 4 * token_count * top_count // (3 * experts)
    weight_blocks = gather_rows(w_gate_up[0], "dp", block_rows)
    ordered = []
    for block in range(replicas):
        chosen_block = weight_blocks[0][1]
        for index, weight in weight_blocks[1:]:
            chosen_block = jnp.where(index == block, weight, chosen_block)
        ordered.append(chosen_block)
    weight_fwd = jnp.concatenate(ordered, axis=0)
    flat_routes = expert_ids.reshape(token_count * top_count)
    onehot = (flat_routes[:, None] == jnp.arange(experts, dtype=jnp.int32)[None, :]).astype(
        jnp.int32
    )
    before = jnp.cumsum(onehot, axis=0) - onehot
    slot_rank = jnp.sum(before * onehot, axis=1)
    target_rows = flat_routes * capacity + slot_rank
    slots = jnp.arange(experts * capacity, dtype=jnp.int32)
    chosen = target_rows.reshape(token_count, top_count)[None, :, :] == slots[:, None, None]
    pick = jnp.any(chosen, axis=2).astype(jnp.bfloat16)
    slot_prob = jnp.sum(jnp.where(chosen, gate_probs[None, :, :], 0.0), axis=(1, 2))
    picked = jnp.dot(
        pick, jnp.concatenate([tokens, cotangent], axis=1), preferred_element_type=jnp.float32
    )
    columns = lax.broadcasted_iota(jnp.int32, picked.shape, 1)
    scale = jnp.where(columns < model_width, 1.0, slot_prob[:, None])
    both_send = (picked * scale).astype(jnp.bfloat16)
    both_recv = lax.all_to_all(
        both_send.reshape(experts, capacity, 2 * model_width),
        "expert",
        split_axis=0,
        concat_axis=0,
        tiled=True,
    ).reshape(experts * capacity, 2 * model_width)
    input_rows = both_recv[:, :model_width]
    cot_rows = both_recv[:, model_width:]
    weight_down = w_down[0]


    gate_up = jnp.dot(input_rows, weight_fwd, preferred_element_type=jnp.float32)
    gate = gate_up[:, :hidden_units]
    upper = gate_up[:, hidden_units:]
    sigma = jax.nn.sigmoid(gate)
    active = gate * sigma
    hidden = (active * upper).astype(jnp.bfloat16)
    output_rows = jnp.dot(hidden, weight_down, preferred_element_type=jnp.float32).astype(
        jnp.bfloat16
    )
    hidden_grad = lax.dot_general(
        cot_rows, weight_down, (((1,), (1,)), ((), ())), preferred_element_type=jnp.float32
    )
    gate_cot = hidden_grad * upper * sigma * (1.0 + gate * (1.0 - sigma))
    upper_cot = hidden_grad * active
    pair_cot = jnp.concatenate([gate_cot, upper_cot], axis=1).astype(jnp.bfloat16)
    send_back = jnp.zeros((experts * capacity, 2 * model_width), jnp.bfloat16)
    send_back = lax.dynamic_update_slice_in_dim(send_back, output_rows, 0, axis=1)
    input_cot = lax.dot_general(
        pair_cot, weight_fwd, (((1,), (1,)), ((), ())), preferred_element_type=jnp.float32
    ).astype(jnp.bfloat16)
    send_back = lax.dynamic_update_slice_in_dim(
        send_back, input_cot, model_width + jnp.minimum(me_dp, 0), axis=1
    )
    back = lax.all_to_all(
        send_back.reshape(
            experts, capacity, 2 * model_width
        ),
        "expert",
        split_axis=0,
        concat_axis=0,
        tiled=True,
    ).reshape(experts * capacity, 2 * model_width)
    owned = (target_rows.reshape(token_count * top_count)[:, None] == slots[None, :]).astype(
        jnp.bfloat16
    )
    slot_both = jnp.dot(owned, back, preferred_element_type=jnp.float32).reshape(
        token_count, top_count, 2 * model_width
    )
    slot_out = slot_both[:, :, :model_width]
    slot_in = slot_both[:, :, model_width:]
    layer_out = jnp.sum(gate_probs[:, :, None] * slot_out, axis=1).astype(jnp.bfloat16)
    input_grad = jnp.sum(slot_in, axis=1).astype(jnp.bfloat16)
    prob_grad = jnp.sum(cotangent[:, None, :].astype(jnp.float32) * slot_out, axis=2)
    weight_cot = lax.dot_general(
        input_rows, pair_cot, (((0,), (0,)), ((), ())), preferred_element_type=jnp.float32
    )

    def grad_block(block):
        return lax.dynamic_slice_in_dim(weight_cot, block * block_rows, block_rows, axis=0)

    grad_rows = grad_block(me_dp)
    for shift in range(1, replicas):
        moved = lax.ppermute(
            grad_block((me_dp + shift) % replicas).astype(jnp.bfloat16),
            "dp",
            [(i, (i + shift) % replicas) for i in range(replicas)],
        )
        grad_rows = grad_rows + moved.astype(jnp.float32)
    return (layer_out, input_grad, prob_grad, grad_rows.astype(jnp.bfloat16)[None])


def solution(mesh):
    placed = (
        P(("dp", "expert"), None),
        P(("dp", "expert"), None),
        P(("dp", "expert"), None),
        P(("dp", "expert"), None),
        P("expert", "dp", None),
        P("expert", None, None),
    )
    return jax.shard_map(
        local,
        mesh=mesh,
        in_specs=placed,
        out_specs=(
            P(("dp", "expert"), None),
            P(("dp", "expert"), None),
            P(("dp", "expert"), None),
            P("expert", "dp", None),
        ),
        check_vma=False,
    )
```

```python
import jax
import jax.numpy as jnp
from jax import lax
from jax.sharding import PartitionSpec as P


def gather_rows(own, axis_name, width):
    count = lax.axis_size(axis_name)
    me = lax.axis_index(axis_name)
    pieces = [(me, own)]
    for shift in range(1, count):
        moved = lax.ppermute(own, axis_name, [(i, (i + shift) % count) for i in range(count)])
        pieces.append(((me - shift) % count, moved))
    return pieces


def local(tokens, cotangent, expert_ids, gate_probs, w_gate_up, w_down):
    experts = lax.axis_size("expert")
    replicas = lax.axis_size("dp")
    me_dp = lax.axis_index("dp")
    token_count = tokens.shape[0]
    model_width = tokens.shape[1]
    top_count = expert_ids.shape[1]
    hidden_units = w_down.shape[1]
    block_rows = w_gate_up.shape[1]
    capacity = 4 * token_count * top_count // (3 * experts)
    weight_blocks = gather_rows(w_gate_up[0], "dp", block_rows)
    ordered = []
    for block in range(replicas):
        chosen_block = weight_blocks[0][1]
        for index, weight in weight_blocks[1:]:
            chosen_block = jnp.where(index == block, weight, chosen_block)
        ordered.append(chosen_block)
    weight_fwd = lax.optimization_barrier(jnp.concatenate(ordered, axis=0))
    flat_routes = expert_ids.reshape(token_count * top_count)
    onehot = (flat_routes[:, None] == jnp.arange(experts, dtype=jnp.int32)[None, :]).astype(
        jnp.int32
    )
    before = jnp.cumsum(onehot, axis=0) - onehot
    slot_rank = jnp.sum(before * onehot, axis=1)
    target_rows = flat_routes * capacity + slot_rank
    slots = jnp.arange(experts * capacity, dtype=jnp.int32)
    chosen = target_rows.reshape(token_count, top_count)[None, :, :] == slots[:, None, None]
    pick = jnp.any(chosen, axis=2).astype(jnp.bfloat16)
    slot_prob = jnp.sum(jnp.where(chosen, gate_probs[None, :, :], 0.0), axis=(1, 2))
    picked = jnp.dot(
        pick, jnp.concatenate([tokens, cotangent], axis=1), preferred_element_type=jnp.float32
    )
    columns = lax.broadcasted_iota(jnp.int32, picked.shape, 1)
    scale = jnp.where(columns < model_width, 1.0, slot_prob[:, None])
    both_send = (picked * scale).astype(jnp.bfloat16)
    both_recv = lax.all_to_all(
        both_send.reshape(experts, capacity, 2 * model_width),
        "expert",
        split_axis=0,
        concat_axis=0,
        tiled=True,
    ).reshape(experts * capacity, 2 * model_width)
    input_rows = both_recv[:, :model_width]
    cot_rows = both_recv[:, model_width:]
    weight_down = w_down[0]


    gate_up = jnp.dot(input_rows, weight_fwd, preferred_element_type=jnp.float32)
    gate = gate_up[:, :hidden_units]
    upper = gate_up[:, hidden_units:]
    sigma = jax.nn.sigmoid(gate)
    active = gate * sigma
    hidden = (active * upper).astype(jnp.bfloat16)
    output_rows = jnp.dot(hidden, weight_down, preferred_element_type=jnp.float32).astype(
        jnp.bfloat16
    )
    hidden_grad = lax.dot_general(
        cot_rows, weight_down, (((1,), (1,)), ((), ())), preferred_element_type=jnp.float32
    )
    gate_cot = hidden_grad * upper * sigma * (1.0 + gate * (1.0 - sigma))
    upper_cot = hidden_grad * active
    pair_cot = jnp.concatenate([gate_cot, upper_cot], axis=1).astype(jnp.bfloat16)
    send_back = jnp.zeros((experts * capacity, 2 * model_width), jnp.bfloat16)
    send_back = lax.dynamic_update_slice_in_dim(send_back, output_rows, 0, axis=1)
    for block, weight in weight_blocks:
        part = lax.dot_general(
            pair_cot, weight, (((1,), (1,)), ((), ())), preferred_element_type=jnp.float32
        ).astype(jnp.bfloat16)
        send_back = lax.dynamic_update_slice_in_dim(
            send_back, part, model_width + block * block_rows, axis=1
        )
    back = lax.all_to_all(
        send_back.reshape(
            experts, capacity, 2 * model_width
        ),
        "expert",
        split_axis=0,
        concat_axis=0,
        tiled=True,
    ).reshape(experts * capacity, 2 * model_width)
    owned = (target_rows.reshape(token_count * top_count)[:, None] == slots[None, :]).astype(
        jnp.bfloat16
    )
    slot_both = jnp.dot(owned, back, preferred_element_type=jnp.float32).reshape(
        token_count, top_count, 2 * model_width
    )
    slot_out = slot_both[:, :, :model_width]
    slot_in = slot_both[:, :, model_width:]
    layer_out = jnp.sum(gate_probs[:, :, None] * slot_out, axis=1).astype(jnp.bfloat16)
    input_grad = jnp.sum(slot_in, axis=1).astype(jnp.bfloat16)
    prob_grad = jnp.sum(cotangent[:, None, :].astype(jnp.float32) * slot_out, axis=2)
    weight_cot = lax.dot_general(
        input_rows, pair_cot, (((0,), (0,)), ((), ())), preferred_element_type=jnp.float32
    )

    def grad_block(block):
        return lax.dynamic_slice_in_dim(weight_cot, block * block_rows, block_rows, axis=0)

    grad_rows = grad_block(me_dp)
    for shift in range(1, replicas):
        moved = lax.ppermute(
            grad_block((me_dp + shift) % replicas).astype(jnp.bfloat16),
            "dp",
            [(i, (i + shift) % replicas) for i in range(replicas)],
        )
        grad_rows = grad_rows + moved.astype(jnp.float32)
    return (layer_out, input_grad, prob_grad, grad_rows.astype(jnp.bfloat16)[None])


def solution(mesh):
    placed = (
        P(("dp", "expert"), None),
        P(("dp", "expert"), None),
        P(("dp", "expert"), None),
        P(("dp", "expert"), None),
        P("expert", "dp", None),
        P("expert", None, None),
    )
    return jax.shard_map(
        local,
        mesh=mesh,
        in_specs=placed,
        out_specs=(
            P(("dp", "expert"), None),
            P(("dp", "expert"), None),
            P(("dp", "expert"), None),
            P("expert", "dp", None),
        ),
        check_vma=False,
    )
```

```python
import jax
import jax.numpy as jnp
from jax import lax
from jax.sharding import PartitionSpec as P


def gather_rows(own, axis_name, width):
    count = lax.axis_size(axis_name)
    me = lax.axis_index(axis_name)
    pieces = [(me, own)]
    for shift in range(1, count):
        moved = lax.ppermute(own, axis_name, [(i, (i + shift) % count) for i in range(count)])
        pieces.append(((me - shift) % count, moved))
    return pieces


def local(tokens, cotangent, expert_ids, gate_probs, w_gate_up, w_down):
    experts = lax.axis_size("expert")
    replicas = lax.axis_size("dp")
    me_dp = lax.axis_index("dp")
    token_count = tokens.shape[0]
    model_width = tokens.shape[1]
    top_count = expert_ids.shape[1]
    hidden_units = w_down.shape[1]
    block_rows = w_gate_up.shape[1]
    capacity = 4 * token_count * top_count // (3 * experts)
    weight_blocks = gather_rows(w_gate_up[0], "dp", block_rows)
    hit = expert_ids[:, :, None] == jnp.arange(experts, dtype=jnp.int32)[None, None, :]
    token_hit = jnp.any(hit, axis=1)
    token_prob = jnp.sum(jnp.where(hit, gate_probs[:, :, None], 0.0), axis=1)
    earlier = (
        lax.broadcasted_iota(jnp.int32, (token_count, token_count), 0)
        > lax.broadcasted_iota(jnp.int32, (token_count, token_count), 1)
    ).astype(jnp.bfloat16)
    rank = jnp.dot(
        earlier, token_hit.astype(jnp.bfloat16), preferred_element_type=jnp.float32
    ).astype(jnp.int32)
    slot_rank = jnp.sum(jnp.where(hit, rank[:, None, :], 0), axis=2)
    target_rows = expert_ids * capacity + slot_rank
    slots = jnp.arange(experts * capacity, dtype=jnp.int32)
    chosen = token_hit.T[:, None, :] & (
        rank.T[:, None, :] == jnp.arange(capacity, dtype=jnp.int32)[None, :, None]
    )
    pick = chosen.reshape(experts * capacity, token_count).astype(jnp.bfloat16)
    slot_prob = jnp.sum(jnp.where(chosen, token_prob.T[:, None, :], 0.0), axis=2).reshape(
        experts * capacity
    )
    picked = jnp.dot(
        pick, jnp.concatenate([tokens, cotangent], axis=1), preferred_element_type=jnp.float32
    )
    columns = lax.broadcasted_iota(jnp.int32, picked.shape, 1)
    scale = jnp.where(columns < model_width, 1.0, slot_prob[:, None])
    both_send = (picked * scale).astype(jnp.bfloat16)
    both_recv = lax.all_to_all(
        both_send.reshape(experts, capacity, 2 * model_width),
        "expert",
        split_axis=0,
        concat_axis=0,
        tiled=True,
    ).reshape(experts * capacity, 2 * model_width)
    input_rows = both_recv[:, :model_width]
    cot_rows = both_recv[:, model_width:]
    weight_down = w_down[0]


    def cols(block):
        return lax.dynamic_slice_in_dim(input_rows, block * block_rows, block_rows, axis=1)

    gate_up = None
    for block, weight in weight_blocks:
        part = jnp.dot(cols(block), weight, preferred_element_type=jnp.float32)
        gate_up = part if gate_up is None else gate_up + part
    gate = gate_up[:, :hidden_units]
    upper = gate_up[:, hidden_units:]
    sigma = jax.nn.sigmoid(gate)
    active = gate * sigma
    hidden = (active * upper).astype(jnp.bfloat16)
    output_rows = jnp.dot(hidden, weight_down, preferred_element_type=jnp.float32).astype(
        jnp.bfloat16
    )
    hidden_grad = lax.dot_general(
        cot_rows, weight_down, (((1,), (1,)), ((), ())), preferred_element_type=jnp.float32
    )
    gate_cot = hidden_grad * upper * sigma * (1.0 + gate * (1.0 - sigma))
    upper_cot = hidden_grad * active
    pair_cot = jnp.concatenate([gate_cot, upper_cot], axis=1).astype(jnp.bfloat16)
    send_back = jnp.zeros((experts * capacity, 2 * model_width), jnp.bfloat16)
    send_back = lax.dynamic_update_slice_in_dim(send_back, output_rows, 0, axis=1)
    for block, weight in weight_blocks:
        part = lax.dot_general(
            pair_cot, weight, (((1,), (1,)), ((), ())), preferred_element_type=jnp.float32
        ).astype(jnp.bfloat16)
        send_back = lax.dynamic_update_slice_in_dim(
            send_back, part, model_width + block * block_rows, axis=1
        )
    back = lax.all_to_all(
        send_back.reshape(
            experts, capacity, 2 * model_width
        ),
        "expert",
        split_axis=0,
        concat_axis=0,
        tiled=True,
    ).reshape(experts * capacity, 2 * model_width)
    owned = (target_rows.reshape(token_count * top_count)[:, None] == slots[None, :]).astype(
        jnp.bfloat16
    )
    slot_both = jnp.dot(owned, back, preferred_element_type=jnp.float32).reshape(
        token_count, top_count, 2 * model_width
    )
    slot_out = slot_both[:, :, :model_width]
    slot_in = slot_both[:, :, model_width:]
    layer_out = jnp.sum(gate_probs[:, :, None] * slot_out, axis=1).astype(jnp.bfloat16)
    input_grad = jnp.sum(slot_in, axis=1).astype(jnp.bfloat16)
    prob_grad = jnp.sum(cotangent[:, None, :].astype(jnp.float32) * slot_out, axis=2)
    weight_cot = lax.dot_general(
        input_rows, pair_cot, (((0,), (0,)), ((), ())), preferred_element_type=jnp.float32
    )

    def grad_block(block):
        return lax.dynamic_slice_in_dim(weight_cot, block * block_rows, block_rows, axis=0)

    grad_rows = grad_block(me_dp)
    for shift in range(1, replicas):
        moved = lax.ppermute(
            grad_block((me_dp + shift) % replicas).astype(jnp.bfloat16),
            "dp",
            [(i, (i + shift) % replicas) for i in range(replicas)],
        )
        grad_rows = grad_rows + moved.astype(jnp.float32)
    return (layer_out, input_grad, prob_grad, grad_rows.astype(jnp.bfloat16)[None])


def solution(mesh):
    placed = (
        P(("dp", "expert"), None),
        P(("dp", "expert"), None),
        P(("dp", "expert"), None),
        P(("dp", "expert"), None),
        P("expert", "dp", None),
        P("expert", None, None),
    )
    return jax.shard_map(
        local,
        mesh=mesh,
        in_specs=placed,
        out_specs=(
            P(("dp", "expert"), None),
            P(("dp", "expert"), None),
            P(("dp", "expert"), None),
            P("expert", "dp", None),
        ),
        check_vma=False,
    )
```

```python
import jax
import jax.numpy as jnp
from jax import lax
from jax.sharding import PartitionSpec as P


def gather_rows(own, axis_name, width):
    count = lax.axis_size(axis_name)
    me = lax.axis_index(axis_name)
    moved = [
        lax.ppermute(own, axis_name, [(i, (i + shift) % count) for i in range(count)])
        for shift in range(1, count)
    ]
    held = lax.optimization_barrier((own, *moved))
    return [((me - shift) % count, block) for shift, block in enumerate(held)]


def local(tokens, cotangent, expert_ids, gate_probs, w_gate_up, w_down):
    experts = lax.axis_size("expert")
    replicas = lax.axis_size("dp")
    me_dp = lax.axis_index("dp")
    token_count = tokens.shape[0]
    model_width = tokens.shape[1]
    top_count = expert_ids.shape[1]
    hidden_units = w_down.shape[1]
    block_rows = w_gate_up.shape[1]
    capacity = 4 * token_count * top_count // (3 * experts)
    weight_blocks = gather_rows(w_gate_up[0], "dp", block_rows)
    hit = expert_ids[:, :, None] == jnp.arange(experts, dtype=jnp.int32)[None, None, :]
    token_hit = jnp.any(hit, axis=1)
    token_prob = jnp.sum(jnp.where(hit, gate_probs[:, :, None], 0.0), axis=1)
    earlier = (
        lax.broadcasted_iota(jnp.int32, (token_count, token_count), 0)
        > lax.broadcasted_iota(jnp.int32, (token_count, token_count), 1)
    ).astype(jnp.bfloat16)
    rank = jnp.dot(
        earlier, token_hit.astype(jnp.bfloat16), preferred_element_type=jnp.float32
    ).astype(jnp.int32)
    slot_rank = jnp.sum(jnp.where(hit, rank[:, None, :], 0), axis=2)
    target_rows = expert_ids * capacity + slot_rank
    slots = jnp.arange(experts * capacity, dtype=jnp.int32)
    chosen = token_hit.T[:, None, :] & (
        rank.T[:, None, :] == jnp.arange(capacity, dtype=jnp.int32)[None, :, None]
    )
    pick = chosen.reshape(experts * capacity, token_count).astype(jnp.bfloat16)
    slot_prob = jnp.sum(jnp.where(chosen, token_prob.T[:, None, :], 0.0), axis=2).reshape(
        experts * capacity
    )
    picked = jnp.dot(
        pick, jnp.concatenate([tokens, cotangent], axis=1), preferred_element_type=jnp.float32
    )
    columns = lax.broadcasted_iota(jnp.int32, picked.shape, 1)
    scale = jnp.where(columns < model_width, 1.0, slot_prob[:, None])
    both_send = (picked * scale).astype(jnp.bfloat16)
    both_recv = lax.all_to_all(
        both_send.reshape(experts, capacity, 2 * model_width),
        "expert",
        split_axis=0,
        concat_axis=0,
        tiled=True,
    ).reshape(experts * capacity, 2 * model_width)
    input_rows = both_recv[:, :model_width]
    cot_rows = both_recv[:, model_width:]
    weight_down = w_down[0]


    def cols(block):
        return lax.dynamic_slice_in_dim(input_rows, block * block_rows, block_rows, axis=1)

    gate_up = None
    for block, weight in weight_blocks:
        part = jnp.dot(cols(block), weight, preferred_element_type=jnp.float32)
        gate_up = part if gate_up is None else gate_up + part
    gate = gate_up[:, :hidden_units]
    upper = gate_up[:, hidden_units:]
    sigma = jax.nn.sigmoid(gate)
    active = gate * sigma
    hidden = (active * upper).astype(jnp.bfloat16)
    output_rows = jnp.dot(hidden, weight_down, preferred_element_type=jnp.float32).astype(
        jnp.bfloat16
    )
    hidden_grad = lax.dot_general(
        cot_rows, weight_down, (((1,), (1,)), ((), ())), preferred_element_type=jnp.float32
    )
    gate_cot = hidden_grad * upper * sigma * (1.0 + gate * (1.0 - sigma))
    upper_cot = hidden_grad * active
    pair_cot = jnp.concatenate([gate_cot, upper_cot], axis=1).astype(jnp.bfloat16)
    send_back = jnp.zeros((experts * capacity, 2 * model_width), jnp.bfloat16)
    send_back = lax.dynamic_update_slice_in_dim(send_back, output_rows, 0, axis=1)
    for block, weight in weight_blocks:
        part = lax.dot_general(
            pair_cot, weight, (((1,), (1,)), ((), ())), preferred_element_type=jnp.float32
        ).astype(jnp.bfloat16)
        send_back = lax.dynamic_update_slice_in_dim(
            send_back, part, model_width + block * block_rows, axis=1
        )
    back = lax.all_to_all(
        send_back.reshape(
            experts, capacity, 2 * model_width
        ),
        "expert",
        split_axis=0,
        concat_axis=0,
        tiled=True,
    ).reshape(experts * capacity, 2 * model_width)
    owned = (target_rows.reshape(token_count * top_count)[:, None] == slots[None, :]).astype(
        jnp.bfloat16
    )
    slot_both = jnp.dot(owned, back, preferred_element_type=jnp.float32).reshape(
        token_count, top_count, 2 * model_width
    )
    slot_out = slot_both[:, :, :model_width]
    slot_in = slot_both[:, :, model_width:]
    layer_out = jnp.sum(gate_probs[:, :, None] * slot_out, axis=1).astype(jnp.bfloat16)
    input_grad = jnp.sum(slot_in, axis=1).astype(jnp.bfloat16)
    prob_grad = jnp.sum(cotangent[:, None, :].astype(jnp.float32) * slot_out, axis=2)
    weight_cot = lax.dot_general(
        input_rows, pair_cot, (((0,), (0,)), ((), ())), preferred_element_type=jnp.float32
    )

    def grad_block(block):
        return lax.dynamic_slice_in_dim(weight_cot, block * block_rows, block_rows, axis=0)

    grad_rows = grad_block(me_dp)
    for shift in range(1, replicas):
        moved = lax.ppermute(
            grad_block((me_dp + shift) % replicas).astype(jnp.bfloat16),
            "dp",
            [(i, (i + shift) % replicas) for i in range(replicas)],
        )
        grad_rows = grad_rows + moved.astype(jnp.float32)
    return (layer_out, input_grad, prob_grad, grad_rows.astype(jnp.bfloat16)[None])


def solution(mesh):
    placed = (
        P(("dp", "expert"), None),
        P(("dp", "expert"), None),
        P(("dp", "expert"), None),
        P(("dp", "expert"), None),
        P("expert", "dp", None),
        P("expert", None, None),
    )
    return jax.shard_map(
        local,
        mesh=mesh,
        in_specs=placed,
        out_specs=(
            P(("dp", "expert"), None),
            P(("dp", "expert"), None),
            P(("dp", "expert"), None),
            P("expert", "dp", None),
        ),
        check_vma=False,
    )
```

```python
import jax
import jax.numpy as jnp
from jax import lax
from jax.sharding import PartitionSpec as P


def gather_rows(own, axis_name, width):
    count = lax.axis_size(axis_name)
    me = lax.axis_index(axis_name)
    moved = [
        lax.ppermute(own, axis_name, [(i, (i + shift) % count) for i in range(count)])
        for shift in range(1, count)
    ]
    held = lax.optimization_barrier((own, *moved))
    keep = me >= 0
    fresh = lax.optimization_barrier(
        tuple(jnp.where(keep, block, jnp.zeros_like(block)) for block in held)
    )
    return [((me - shift) % count, block) for shift, block in enumerate(fresh)]


def local(tokens, cotangent, expert_ids, gate_probs, w_gate_up, w_down):
    experts = lax.axis_size("expert")
    replicas = lax.axis_size("dp")
    me_dp = lax.axis_index("dp")
    token_count = tokens.shape[0]
    model_width = tokens.shape[1]
    top_count = expert_ids.shape[1]
    hidden_units = w_down.shape[1]
    block_rows = w_gate_up.shape[1]
    capacity = 4 * token_count * top_count // (3 * experts)
    weight_blocks = gather_rows(w_gate_up[0], "dp", block_rows)
    hit = expert_ids[:, :, None] == jnp.arange(experts, dtype=jnp.int32)[None, None, :]
    token_hit = jnp.any(hit, axis=1)
    token_prob = jnp.sum(jnp.where(hit, gate_probs[:, :, None], 0.0), axis=1)
    earlier = (
        lax.broadcasted_iota(jnp.int32, (token_count, token_count), 0)
        > lax.broadcasted_iota(jnp.int32, (token_count, token_count), 1)
    ).astype(jnp.bfloat16)
    rank = jnp.dot(
        earlier, token_hit.astype(jnp.bfloat16), preferred_element_type=jnp.float32
    ).astype(jnp.int32)
    slot_rank = jnp.sum(jnp.where(hit, rank[:, None, :], 0), axis=2)
    target_rows = expert_ids * capacity + slot_rank
    slots = jnp.arange(experts * capacity, dtype=jnp.int32)
    chosen = token_hit.T[:, None, :] & (
        rank.T[:, None, :] == jnp.arange(capacity, dtype=jnp.int32)[None, :, None]
    )
    pick = chosen.reshape(experts * capacity, token_count).astype(jnp.bfloat16)
    slot_prob = jnp.sum(jnp.where(chosen, token_prob.T[:, None, :], 0.0), axis=2).reshape(
        experts * capacity
    )
    picked = jnp.dot(
        pick, jnp.concatenate([tokens, cotangent], axis=1), preferred_element_type=jnp.float32
    )
    columns = lax.broadcasted_iota(jnp.int32, picked.shape, 1)
    scale = jnp.where(columns < model_width, 1.0, slot_prob[:, None])
    both_send = (picked * scale).astype(jnp.bfloat16)
    both_recv = lax.all_to_all(
        both_send.reshape(experts, capacity, 2 * model_width),
        "expert",
        split_axis=0,
        concat_axis=0,
        tiled=True,
    ).reshape(experts * capacity, 2 * model_width)
    input_rows = both_recv[:, :model_width]
    cot_rows = both_recv[:, model_width:]
    weight_down = w_down[0]


    def cols(block):
        return lax.dynamic_slice_in_dim(input_rows, block * block_rows, block_rows, axis=1)

    gate_up = None
    for block, weight in weight_blocks:
        part = jnp.dot(cols(block), weight, preferred_element_type=jnp.float32)
        gate_up = part if gate_up is None else gate_up + part
    gate = gate_up[:, :hidden_units]
    upper = gate_up[:, hidden_units:]
    sigma = jax.nn.sigmoid(gate)
    active = gate * sigma
    hidden = (active * upper).astype(jnp.bfloat16)
    output_rows = jnp.dot(hidden, weight_down, preferred_element_type=jnp.float32).astype(
        jnp.bfloat16
    )
    hidden_grad = lax.dot_general(
        cot_rows, weight_down, (((1,), (1,)), ((), ())), preferred_element_type=jnp.float32
    )
    gate_cot = hidden_grad * upper * sigma * (1.0 + gate * (1.0 - sigma))
    upper_cot = hidden_grad * active
    pair_cot = jnp.concatenate([gate_cot, upper_cot], axis=1).astype(jnp.bfloat16)
    send_back = jnp.zeros((experts * capacity, 2 * model_width), jnp.bfloat16)
    send_back = lax.dynamic_update_slice_in_dim(send_back, output_rows, 0, axis=1)
    for block, weight in weight_blocks:
        part = lax.dot_general(
            pair_cot, weight, (((1,), (1,)), ((), ())), preferred_element_type=jnp.float32
        ).astype(jnp.bfloat16)
        send_back = lax.dynamic_update_slice_in_dim(
            send_back, part, model_width + block * block_rows, axis=1
        )
    back = lax.all_to_all(
        send_back.reshape(
            experts, capacity, 2 * model_width
        ),
        "expert",
        split_axis=0,
        concat_axis=0,
        tiled=True,
    ).reshape(experts * capacity, 2 * model_width)
    owned = (target_rows.reshape(token_count * top_count)[:, None] == slots[None, :]).astype(
        jnp.bfloat16
    )
    slot_both = jnp.dot(owned, back, preferred_element_type=jnp.float32).reshape(
        token_count, top_count, 2 * model_width
    )
    slot_out = slot_both[:, :, :model_width]
    slot_in = slot_both[:, :, model_width:]
    layer_out = jnp.sum(gate_probs[:, :, None] * slot_out, axis=1).astype(jnp.bfloat16)
    input_grad = jnp.sum(slot_in, axis=1).astype(jnp.bfloat16)
    prob_grad = jnp.sum(cotangent[:, None, :].astype(jnp.float32) * slot_out, axis=2)
    weight_cot = lax.dot_general(
        input_rows, pair_cot, (((0,), (0,)), ((), ())), preferred_element_type=jnp.float32
    )

    def grad_block(block):
        return lax.dynamic_slice_in_dim(weight_cot, block * block_rows, block_rows, axis=0)

    grad_rows = grad_block(me_dp)
    for shift in range(1, replicas):
        moved = lax.ppermute(
            grad_block((me_dp + shift) % replicas).astype(jnp.bfloat16),
            "dp",
            [(i, (i + shift) % replicas) for i in range(replicas)],
        )
        grad_rows = grad_rows + moved.astype(jnp.float32)
    return (layer_out, input_grad, prob_grad, grad_rows.astype(jnp.bfloat16)[None])


def solution(mesh):
    placed = (
        P(("dp", "expert"), None),
        P(("dp", "expert"), None),
        P(("dp", "expert"), None),
        P(("dp", "expert"), None),
        P("expert", "dp", None),
        P("expert", None, None),
    )
    return jax.shard_map(
        local,
        mesh=mesh,
        in_specs=placed,
        out_specs=(
            P(("dp", "expert"), None),
            P(("dp", "expert"), None),
            P(("dp", "expert"), None),
            P("expert", "dp", None),
        ),
        check_vma=False,
    )
```

```python
import jax
import jax.numpy as jnp
from jax import lax
from jax.sharding import PartitionSpec as P


def gather_rows(own, axis_name, width):
    count = lax.axis_size(axis_name)
    me = lax.axis_index(axis_name)
    moved = [
        lax.ppermute(own, axis_name, [(i, (i + shift) % count) for i in range(count)])
        for shift in range(1, count)
    ]
    held = lax.optimization_barrier((own, *moved))
    keep = me >= 0
    fresh = lax.optimization_barrier(
        tuple(jnp.where(keep, block, jnp.zeros_like(block)) for block in held)
    )
    return [((me - shift) % count, block) for shift, block in enumerate(fresh)]


def local(tokens, cotangent, expert_ids, gate_probs, w_gate_up, w_down):
    experts = lax.axis_size("expert")
    replicas = lax.axis_size("dp")
    me_dp = lax.axis_index("dp")
    token_count = tokens.shape[0]
    model_width = tokens.shape[1]
    top_count = expert_ids.shape[1]
    hidden_units = w_down.shape[1]
    block_rows = w_gate_up.shape[1]
    capacity = 4 * token_count * top_count // (3 * experts)
    weight_blocks = gather_rows(w_gate_up[0], "dp", block_rows)
    hit = expert_ids[:, :, None] == jnp.arange(experts, dtype=jnp.int32)[None, None, :]
    token_hit = jnp.any(hit, axis=1)
    token_prob = jnp.sum(jnp.where(hit, gate_probs[:, :, None], 0.0), axis=1)
    earlier = (
        lax.broadcasted_iota(jnp.int32, (token_count, token_count), 0)
        > lax.broadcasted_iota(jnp.int32, (token_count, token_count), 1)
    ).astype(jnp.bfloat16)
    rank = jnp.dot(
        earlier, token_hit.astype(jnp.bfloat16), preferred_element_type=jnp.float32
    ).astype(jnp.int32)
    slot_rank = jnp.sum(jnp.where(hit, rank[:, None, :], 0), axis=2)
    target_rows = expert_ids * capacity + slot_rank
    slots = jnp.arange(experts * capacity, dtype=jnp.int32)
    chosen = token_hit.T[:, None, :] & (
        rank.T[:, None, :] == jnp.arange(capacity, dtype=jnp.int32)[None, :, None]
    )
    pick = chosen.reshape(experts * capacity, token_count).astype(jnp.bfloat16)
    slot_prob = jnp.sum(jnp.where(chosen, token_prob.T[:, None, :], 0.0), axis=2).reshape(
        experts * capacity
    )
    picked = jnp.dot(
        pick, jnp.concatenate([tokens, cotangent], axis=1), preferred_element_type=jnp.float32
    )
    columns = lax.broadcasted_iota(jnp.int32, picked.shape, 1)
    scale = jnp.where(columns < model_width, 1.0, slot_prob[:, None])
    both_send = (picked * scale).astype(jnp.bfloat16)
    both_recv = lax.all_to_all(
        both_send.reshape(experts, capacity, 2 * model_width),
        "expert",
        split_axis=0,
        concat_axis=0,
        tiled=True,
    ).reshape(experts * capacity, 2 * model_width)
    input_rows = both_recv[:, :model_width]
    cot_rows = both_recv[:, model_width:]
    weight_down = w_down[0]


    def cols(block):
        return lax.dynamic_slice_in_dim(input_rows, block * block_rows, block_rows, axis=1)

    hidden_grad = lax.dot_general(
        cot_rows, weight_down, (((1,), (1,)), ((), ())), preferred_element_type=jnp.float32
    )
    hidden_grad, held_weights = lax.optimization_barrier(
        (hidden_grad, tuple(weight for _, weight in weight_blocks))
    )
    weight_blocks = [(index, weight) for (index, _), weight in zip(weight_blocks, held_weights)]
    gate_up = None
    for block, weight in weight_blocks:
        part = jnp.dot(cols(block), weight, preferred_element_type=jnp.float32)
        gate_up = part if gate_up is None else gate_up + part
    gate = gate_up[:, :hidden_units]
    upper = gate_up[:, hidden_units:]
    sigma = jax.nn.sigmoid(gate)
    active = gate * sigma
    hidden = (active * upper).astype(jnp.bfloat16)
    output_rows = jnp.dot(hidden, weight_down, preferred_element_type=jnp.float32).astype(
        jnp.bfloat16
    )
    gate_cot = hidden_grad * upper * sigma * (1.0 + gate * (1.0 - sigma))
    upper_cot = hidden_grad * active
    pair_cot = jnp.concatenate([gate_cot, upper_cot], axis=1).astype(jnp.bfloat16)
    send_back = jnp.zeros((experts * capacity, 2 * model_width), jnp.bfloat16)
    send_back = lax.dynamic_update_slice_in_dim(send_back, output_rows, 0, axis=1)
    for block, weight in weight_blocks:
        part = lax.dot_general(
            pair_cot, weight, (((1,), (1,)), ((), ())), preferred_element_type=jnp.float32
        ).astype(jnp.bfloat16)
        send_back = lax.dynamic_update_slice_in_dim(
            send_back, part, model_width + block * block_rows, axis=1
        )
    back = lax.all_to_all(
        send_back.reshape(
            experts, capacity, 2 * model_width
        ),
        "expert",
        split_axis=0,
        concat_axis=0,
        tiled=True,
    ).reshape(experts * capacity, 2 * model_width)
    owned = (target_rows.reshape(token_count * top_count)[:, None] == slots[None, :]).astype(
        jnp.bfloat16
    )
    slot_both = jnp.dot(owned, back, preferred_element_type=jnp.float32).reshape(
        token_count, top_count, 2 * model_width
    )
    slot_out = slot_both[:, :, :model_width]
    slot_in = slot_both[:, :, model_width:]
    layer_out = jnp.sum(gate_probs[:, :, None] * slot_out, axis=1).astype(jnp.bfloat16)
    input_grad = jnp.sum(slot_in, axis=1).astype(jnp.bfloat16)
    prob_grad = jnp.sum(cotangent[:, None, :].astype(jnp.float32) * slot_out, axis=2)
    weight_cot = lax.dot_general(
        input_rows, pair_cot, (((0,), (0,)), ((), ())), preferred_element_type=jnp.float32
    )

    def grad_block(block):
        return lax.dynamic_slice_in_dim(weight_cot, block * block_rows, block_rows, axis=0)

    grad_rows = grad_block(me_dp)
    for shift in range(1, replicas):
        moved = lax.ppermute(
            grad_block((me_dp + shift) % replicas).astype(jnp.bfloat16),
            "dp",
            [(i, (i + shift) % replicas) for i in range(replicas)],
        )
        grad_rows = grad_rows + moved.astype(jnp.float32)
    return (layer_out, input_grad, prob_grad, grad_rows.astype(jnp.bfloat16)[None])


def solution(mesh):
    placed = (
        P(("dp", "expert"), None),
        P(("dp", "expert"), None),
        P(("dp", "expert"), None),
        P(("dp", "expert"), None),
        P("expert", "dp", None),
        P("expert", None, None),
    )
    return jax.shard_map(
        local,
        mesh=mesh,
        in_specs=placed,
        out_specs=(
            P(("dp", "expert"), None),
            P(("dp", "expert"), None),
            P(("dp", "expert"), None),
            P("expert", "dp", None),
        ),
        check_vma=False,
    )
```

```python
import jax
import jax.numpy as jnp
from jax import lax
from jax.sharding import PartitionSpec as P


def gather_rows(own, axis_name, width):
    count = lax.axis_size(axis_name)
    me = lax.axis_index(axis_name)
    moved = [
        lax.ppermute(own, axis_name, [(i, (i + shift) % count) for i in range(count)])
        for shift in range(1, count)
    ]
    held = lax.optimization_barrier((own, *moved))
    keep = me >= 0
    fresh = (held[0],) + lax.optimization_barrier(
        tuple(jnp.where(keep, block, jnp.zeros_like(block)) for block in held[1:])
    )
    return [((me - shift) % count, block) for shift, block in enumerate(fresh)]


def local(tokens, cotangent, expert_ids, gate_probs, w_gate_up, w_down):
    experts = lax.axis_size("expert")
    replicas = lax.axis_size("dp")
    me_dp = lax.axis_index("dp")
    token_count = tokens.shape[0]
    model_width = tokens.shape[1]
    top_count = expert_ids.shape[1]
    hidden_units = w_down.shape[1]
    block_rows = w_gate_up.shape[1]
    capacity = 4 * token_count * top_count // (3 * experts)
    weight_blocks = gather_rows(w_gate_up[0], "dp", block_rows)
    hit = expert_ids[:, :, None] == jnp.arange(experts, dtype=jnp.int32)[None, None, :]
    token_hit = jnp.any(hit, axis=1)
    token_prob = jnp.sum(jnp.where(hit, gate_probs[:, :, None], 0.0), axis=1)
    earlier = (
        lax.broadcasted_iota(jnp.int32, (token_count, token_count), 0)
        > lax.broadcasted_iota(jnp.int32, (token_count, token_count), 1)
    ).astype(jnp.bfloat16)
    rank = jnp.dot(
        earlier, token_hit.astype(jnp.bfloat16), preferred_element_type=jnp.float32
    ).astype(jnp.int32)
    slot_rank = jnp.sum(jnp.where(hit, rank[:, None, :], 0), axis=2)
    target_rows = expert_ids * capacity + slot_rank
    slots = jnp.arange(experts * capacity, dtype=jnp.int32)
    chosen = token_hit.T[:, None, :] & (
        rank.T[:, None, :] == jnp.arange(capacity, dtype=jnp.int32)[None, :, None]
    )
    pick = chosen.reshape(experts * capacity, token_count).astype(jnp.bfloat16)
    slot_prob = jnp.sum(jnp.where(chosen, token_prob.T[:, None, :], 0.0), axis=2).reshape(
        experts * capacity
    )
    picked = jnp.dot(
        pick, jnp.concatenate([tokens, cotangent], axis=1), preferred_element_type=jnp.float32
    )
    columns = lax.broadcasted_iota(jnp.int32, picked.shape, 1)
    scale = jnp.where(columns < model_width, 1.0, slot_prob[:, None])
    both_send = (picked * scale).astype(jnp.bfloat16)
    both_recv = lax.all_to_all(
        both_send.reshape(experts, capacity, 2 * model_width),
        "expert",
        split_axis=0,
        concat_axis=0,
        tiled=True,
    ).reshape(experts * capacity, 2 * model_width)
    input_rows = both_recv[:, :model_width]
    cot_rows = both_recv[:, model_width:]
    weight_down = w_down[0]


    def cols(block):
        return lax.dynamic_slice_in_dim(input_rows, block * block_rows, block_rows, axis=1)

    hidden_grad = lax.dot_general(
        cot_rows, weight_down, (((1,), (1,)), ((), ())), preferred_element_type=jnp.float32
    )
    hidden_grad, held_weights = lax.optimization_barrier(
        (hidden_grad, tuple(weight for _, weight in weight_blocks))
    )
    weight_blocks = [(index, weight) for (index, _), weight in zip(weight_blocks, held_weights)]
    gate_up = None
    for block, weight in weight_blocks:
        part = jnp.dot(cols(block), weight, preferred_element_type=jnp.float32)
        gate_up = part if gate_up is None else gate_up + part
    gate = gate_up[:, :hidden_units]
    upper = gate_up[:, hidden_units:]
    sigma = jax.nn.sigmoid(gate)
    active = gate * sigma
    hidden = (active * upper).astype(jnp.bfloat16)
    output_rows = jnp.dot(hidden, weight_down, preferred_element_type=jnp.float32).astype(
        jnp.bfloat16
    )
    gate_cot = hidden_grad * upper * sigma * (1.0 + gate * (1.0 - sigma))
    upper_cot = hidden_grad * active
    pair_cot = jnp.concatenate([gate_cot, upper_cot], axis=1).astype(jnp.bfloat16)
    send_back = jnp.zeros((experts * capacity, 2 * model_width), jnp.bfloat16)
    send_back = lax.dynamic_update_slice_in_dim(send_back, output_rows, 0, axis=1)
    for block, weight in weight_blocks:
        part = lax.dot_general(
            pair_cot, weight, (((1,), (1,)), ((), ())), preferred_element_type=jnp.float32
        ).astype(jnp.bfloat16)
        send_back = lax.dynamic_update_slice_in_dim(
            send_back, part, model_width + block * block_rows, axis=1
        )
    back = lax.all_to_all(
        send_back.reshape(
            experts, capacity, 2 * model_width
        ),
        "expert",
        split_axis=0,
        concat_axis=0,
        tiled=True,
    ).reshape(experts * capacity, 2 * model_width)
    owned = (target_rows.reshape(token_count * top_count)[:, None] == slots[None, :]).astype(
        jnp.bfloat16
    )
    slot_both = jnp.dot(owned, back, preferred_element_type=jnp.float32).reshape(
        token_count, top_count, 2 * model_width
    )
    slot_out = slot_both[:, :, :model_width]
    slot_in = slot_both[:, :, model_width:]
    layer_out = jnp.sum(gate_probs[:, :, None] * slot_out, axis=1).astype(jnp.bfloat16)
    input_grad = jnp.sum(slot_in, axis=1).astype(jnp.bfloat16)
    prob_grad = jnp.sum(cotangent[:, None, :].astype(jnp.float32) * slot_out, axis=2)
    weight_cot = lax.dot_general(
        input_rows, pair_cot, (((0,), (0,)), ((), ())), preferred_element_type=jnp.float32
    )

    def grad_block(block):
        return lax.dynamic_slice_in_dim(weight_cot, block * block_rows, block_rows, axis=0)

    grad_rows = grad_block(me_dp)
    for shift in range(1, replicas):
        moved = lax.ppermute(
            grad_block((me_dp + shift) % replicas).astype(jnp.bfloat16),
            "dp",
            [(i, (i + shift) % replicas) for i in range(replicas)],
        )
        grad_rows = grad_rows + moved.astype(jnp.float32)
    return (layer_out, input_grad, prob_grad, grad_rows.astype(jnp.bfloat16)[None])


def solution(mesh):
    placed = (
        P(("dp", "expert"), None),
        P(("dp", "expert"), None),
        P(("dp", "expert"), None),
        P(("dp", "expert"), None),
        P("expert", "dp", None),
        P("expert", None, None),
    )
    return jax.shard_map(
        local,
        mesh=mesh,
        in_specs=placed,
        out_specs=(
            P(("dp", "expert"), None),
            P(("dp", "expert"), None),
            P(("dp", "expert"), None),
            P("expert", "dp", None),
        ),
        check_vma=False,
    )
```

```python
import jax
import jax.numpy as jnp
from jax import lax
from jax.sharding import PartitionSpec as P


def gather_rows(own, axis_name, width):
    count = lax.axis_size(axis_name)
    me = lax.axis_index(axis_name)
    moved = [
        lax.ppermute(own, axis_name, [(i, (i + shift) % count) for i in range(count)])
        for shift in range(1, count)
    ]
    held = lax.optimization_barrier((own, *moved))
    keep = me >= 0
    fresh = lax.optimization_barrier(
        tuple(jnp.where(keep, block, jnp.zeros_like(block)) for block in held)
    )
    return [((me - shift) % count, block) for shift, block in enumerate(fresh)]


def local(tokens, cotangent, expert_ids, gate_probs, w_gate_up, w_down):
    experts = lax.axis_size("expert")
    replicas = lax.axis_size("dp")
    me_dp = lax.axis_index("dp")
    token_count = tokens.shape[0]
    model_width = tokens.shape[1]
    top_count = expert_ids.shape[1]
    hidden_units = w_down.shape[1]
    block_rows = w_gate_up.shape[1]
    capacity = 4 * token_count * top_count // (3 * experts)
    weight_blocks = gather_rows(w_gate_up[0], "dp", block_rows)
    hit = expert_ids[:, :, None] == jnp.arange(experts, dtype=jnp.int32)[None, None, :]
    token_prob = jnp.sum(jnp.where(hit, gate_probs[:, :, None], 0.0), axis=1)
    token_hit = token_prob > 0.0
    earlier = (
        lax.broadcasted_iota(jnp.int32, (token_count, token_count), 0)
        > lax.broadcasted_iota(jnp.int32, (token_count, token_count), 1)
    ).astype(jnp.bfloat16)
    rank = jnp.dot(
        earlier, token_hit.astype(jnp.bfloat16), preferred_element_type=jnp.float32
    ).astype(jnp.int32)
    slot_rank = jnp.sum(jnp.where(hit, rank[:, None, :], 0), axis=2)
    target_rows = expert_ids * capacity + slot_rank
    slots = jnp.arange(experts * capacity, dtype=jnp.int32)
    chosen = token_hit.T[:, None, :] & (
        rank.T[:, None, :] == jnp.arange(capacity, dtype=jnp.int32)[None, :, None]
    )
    pick = chosen.reshape(experts * capacity, token_count).astype(jnp.bfloat16)
    slot_prob = jnp.sum(jnp.where(chosen, token_prob.T[:, None, :], 0.0), axis=2).reshape(
        experts * capacity
    )
    picked = jnp.dot(
        pick, jnp.concatenate([tokens, cotangent], axis=1), preferred_element_type=jnp.float32
    )
    columns = lax.broadcasted_iota(jnp.int32, picked.shape, 1)
    scale = jnp.where(columns < model_width, 1.0, slot_prob[:, None])
    both_send = (picked * scale).astype(jnp.bfloat16)
    both_recv = lax.all_to_all(
        both_send.reshape(experts, capacity, 2 * model_width),
        "expert",
        split_axis=0,
        concat_axis=0,
        tiled=True,
    ).reshape(experts * capacity, 2 * model_width)
    input_rows = both_recv[:, :model_width]
    cot_rows = both_recv[:, model_width:]
    weight_down = w_down[0]


    def cols(block):
        return lax.dynamic_slice_in_dim(input_rows, block * block_rows, block_rows, axis=1)

    hidden_grad = lax.dot_general(
        cot_rows, weight_down, (((1,), (1,)), ((), ())), preferred_element_type=jnp.float32
    )
    hidden_grad, held_weights = lax.optimization_barrier(
        (hidden_grad, tuple(weight for _, weight in weight_blocks))
    )
    weight_blocks = [(index, weight) for (index, _), weight in zip(weight_blocks, held_weights)]
    gate_up = None
    for block, weight in weight_blocks:
        part = jnp.dot(cols(block), weight, preferred_element_type=jnp.float32)
        gate_up = part if gate_up is None else gate_up + part
    gate = gate_up[:, :hidden_units]
    upper = gate_up[:, hidden_units:]
    sigma = jax.nn.sigmoid(gate)
    active = gate * sigma
    hidden = (active * upper).astype(jnp.bfloat16)
    output_rows = jnp.dot(hidden, weight_down, preferred_element_type=jnp.float32).astype(
        jnp.bfloat16
    )
    gate_cot = hidden_grad * upper * sigma * (1.0 + gate * (1.0 - sigma))
    upper_cot = hidden_grad * active
    pair_cot = jnp.concatenate([gate_cot, upper_cot], axis=1).astype(jnp.bfloat16)
    send_back = jnp.zeros((experts * capacity, 2 * model_width), jnp.bfloat16)
    send_back = lax.dynamic_update_slice_in_dim(send_back, output_rows, 0, axis=1)
    for block, weight in weight_blocks:
        part = lax.dot_general(
            pair_cot, weight, (((1,), (1,)), ((), ())), preferred_element_type=jnp.float32
        ).astype(jnp.bfloat16)
        send_back = lax.dynamic_update_slice_in_dim(
            send_back, part, model_width + block * block_rows, axis=1
        )
    back = lax.all_to_all(
        send_back.reshape(
            experts, capacity, 2 * model_width
        ),
        "expert",
        split_axis=0,
        concat_axis=0,
        tiled=True,
    ).reshape(experts * capacity, 2 * model_width)
    owned = (target_rows.reshape(token_count * top_count)[:, None] == slots[None, :]).astype(
        jnp.bfloat16
    )
    slot_both = jnp.dot(owned, back, preferred_element_type=jnp.float32).reshape(
        token_count, top_count, 2 * model_width
    )
    slot_out = slot_both[:, :, :model_width]
    slot_in = slot_both[:, :, model_width:]
    layer_out = jnp.sum(gate_probs[:, :, None] * slot_out, axis=1).astype(jnp.bfloat16)
    input_grad = jnp.sum(slot_in, axis=1).astype(jnp.bfloat16)
    prob_grad = jnp.sum(cotangent[:, None, :].astype(jnp.float32) * slot_out, axis=2)
    weight_cot = lax.dot_general(
        input_rows, pair_cot, (((0,), (0,)), ((), ())), preferred_element_type=jnp.float32
    )

    def grad_block(block):
        return lax.dynamic_slice_in_dim(weight_cot, block * block_rows, block_rows, axis=0)

    grad_rows = grad_block(me_dp)
    for shift in range(1, replicas):
        moved = lax.ppermute(
            grad_block((me_dp + shift) % replicas).astype(jnp.bfloat16),
            "dp",
            [(i, (i + shift) % replicas) for i in range(replicas)],
        )
        grad_rows = grad_rows + moved.astype(jnp.float32)
    return (layer_out, input_grad, prob_grad, grad_rows.astype(jnp.bfloat16)[None])


def solution(mesh):
    placed = (
        P(("dp", "expert"), None),
        P(("dp", "expert"), None),
        P(("dp", "expert"), None),
        P(("dp", "expert"), None),
        P("expert", "dp", None),
        P("expert", None, None),
    )
    return jax.shard_map(
        local,
        mesh=mesh,
        in_specs=placed,
        out_specs=(
            P(("dp", "expert"), None),
            P(("dp", "expert"), None),
            P(("dp", "expert"), None),
            P("expert", "dp", None),
        ),
        check_vma=False,
    )
```

```python
import jax
import jax.numpy as jnp
from jax import lax
from jax.sharding import PartitionSpec as P


def gather_rows(own, axis_name, width):
    count = lax.axis_size(axis_name)
    me = lax.axis_index(axis_name)
    moved = [
        lax.ppermute(own, axis_name, [(i, (i + shift) % count) for i in range(count)])
        for shift in range(1, count)
    ]
    held = lax.optimization_barrier((own, *moved))
    keep = me >= 0
    fresh = lax.optimization_barrier(
        tuple(jnp.where(keep, block, jnp.zeros_like(block)) for block in held)
    )
    return [((me - shift) % count, block) for shift, block in enumerate(fresh)]


def local(tokens, cotangent, expert_ids, gate_probs, w_gate_up, w_down):
    experts = lax.axis_size("expert")
    replicas = lax.axis_size("dp")
    me_dp = lax.axis_index("dp")
    token_count = tokens.shape[0]
    model_width = tokens.shape[1]
    top_count = expert_ids.shape[1]
    hidden_units = w_down.shape[1]
    block_rows = w_gate_up.shape[1]
    capacity = 4 * token_count * top_count // (3 * experts)
    weight_blocks = gather_rows(w_gate_up[0], "dp", block_rows)
    hit = expert_ids[:, :, None] == jnp.arange(experts, dtype=jnp.int32)[None, None, :]
    token_prob = jnp.sum(jnp.where(hit, gate_probs[:, :, None], 0.0), axis=1)
    token_hit = token_prob > 0.0
    earlier = (
        lax.broadcasted_iota(jnp.int32, (token_count, token_count), 0)
        > lax.broadcasted_iota(jnp.int32, (token_count, token_count), 1)
    ).astype(jnp.bfloat16)
    rank = jnp.dot(
        earlier, token_hit.astype(jnp.bfloat16), preferred_element_type=jnp.float32
    ).astype(jnp.int32)
    slot_rank = jnp.sum(jnp.where(hit, rank[:, None, :], 0), axis=2)
    target_rows = expert_ids * capacity + slot_rank
    slots = jnp.arange(experts * capacity, dtype=jnp.int32)
    chosen = token_hit.T[:, None, :] & (
        rank.T[:, None, :] == jnp.arange(capacity, dtype=jnp.int32)[None, :, None]
    )
    pick = chosen.reshape(experts * capacity, token_count).astype(jnp.bfloat16)
    slot_prob = jnp.sum(jnp.where(chosen, token_prob.T[:, None, :], 0.0), axis=2).reshape(
        experts * capacity
    )
    rows_both = lax.optimization_barrier(jnp.concatenate([tokens, cotangent], axis=1))
    picked = jnp.dot(pick, rows_both, preferred_element_type=jnp.float32)
    columns = lax.broadcasted_iota(jnp.int32, picked.shape, 1)
    scale = jnp.where(columns < model_width, 1.0, slot_prob[:, None])
    both_send = (picked * scale).astype(jnp.bfloat16)
    both_recv = lax.all_to_all(
        both_send.reshape(experts, capacity, 2 * model_width),
        "expert",
        split_axis=0,
        concat_axis=0,
        tiled=True,
    ).reshape(experts * capacity, 2 * model_width)
    input_rows = both_recv[:, :model_width]
    cot_rows = both_recv[:, model_width:]
    weight_down = w_down[0]


    def cols(block):
        return lax.dynamic_slice_in_dim(input_rows, block * block_rows, block_rows, axis=1)

    hidden_grad = lax.dot_general(
        cot_rows, weight_down, (((1,), (1,)), ((), ())), preferred_element_type=jnp.float32
    )
    hidden_grad, held_weights = lax.optimization_barrier(
        (hidden_grad, tuple(weight for _, weight in weight_blocks))
    )
    weight_blocks = [(index, weight) for (index, _), weight in zip(weight_blocks, held_weights)]
    gate_up = None
    for block, weight in weight_blocks:
        part = jnp.dot(cols(block), weight, preferred_element_type=jnp.float32)
        gate_up = part if gate_up is None else gate_up + part
    gate = gate_up[:, :hidden_units]
    upper = gate_up[:, hidden_units:]
    sigma = jax.nn.sigmoid(gate)
    active = gate * sigma
    hidden = (active * upper).astype(jnp.bfloat16)
    output_rows = jnp.dot(hidden, weight_down, preferred_element_type=jnp.float32).astype(
        jnp.bfloat16
    )
    gate_cot = hidden_grad * upper * sigma * (1.0 + gate * (1.0 - sigma))
    upper_cot = hidden_grad * active
    pair_cot = jnp.concatenate([gate_cot, upper_cot], axis=1).astype(jnp.bfloat16)
    send_back = jnp.zeros((experts * capacity, 2 * model_width), jnp.bfloat16)
    send_back = lax.dynamic_update_slice_in_dim(send_back, output_rows, 0, axis=1)
    for block, weight in weight_blocks:
        part = lax.dot_general(
            pair_cot, weight, (((1,), (1,)), ((), ())), preferred_element_type=jnp.float32
        ).astype(jnp.bfloat16)
        send_back = lax.dynamic_update_slice_in_dim(
            send_back, part, model_width + block * block_rows, axis=1
        )
    back = lax.all_to_all(
        send_back.reshape(
            experts, capacity, 2 * model_width
        ),
        "expert",
        split_axis=0,
        concat_axis=0,
        tiled=True,
    ).reshape(experts * capacity, 2 * model_width)
    owned = (target_rows.reshape(token_count * top_count)[:, None] == slots[None, :]).astype(
        jnp.bfloat16
    )
    slot_both = jnp.dot(owned, back, preferred_element_type=jnp.float32).reshape(
        token_count, top_count, 2 * model_width
    )
    slot_out = slot_both[:, :, :model_width]
    slot_in = slot_both[:, :, model_width:]
    layer_out = jnp.sum(gate_probs[:, :, None] * slot_out, axis=1).astype(jnp.bfloat16)
    input_grad = jnp.sum(slot_in, axis=1).astype(jnp.bfloat16)
    prob_grad = jnp.sum(cotangent[:, None, :].astype(jnp.float32) * slot_out, axis=2)
    weight_cot = lax.dot_general(
        input_rows, pair_cot, (((0,), (0,)), ((), ())), preferred_element_type=jnp.float32
    )

    def grad_block(block):
        return lax.dynamic_slice_in_dim(weight_cot, block * block_rows, block_rows, axis=0)

    grad_rows = grad_block(me_dp)
    for shift in range(1, replicas):
        moved = lax.ppermute(
            grad_block((me_dp + shift) % replicas).astype(jnp.bfloat16),
            "dp",
            [(i, (i + shift) % replicas) for i in range(replicas)],
        )
        grad_rows = grad_rows + moved.astype(jnp.float32)
    return (layer_out, input_grad, prob_grad, grad_rows.astype(jnp.bfloat16)[None])


def solution(mesh):
    placed = (
        P(("dp", "expert"), None),
        P(("dp", "expert"), None),
        P(("dp", "expert"), None),
        P(("dp", "expert"), None),
        P("expert", "dp", None),
        P("expert", None, None),
    )
    return jax.shard_map(
        local,
        mesh=mesh,
        in_specs=placed,
        out_specs=(
            P(("dp", "expert"), None),
            P(("dp", "expert"), None),
            P(("dp", "expert"), None),
            P("expert", "dp", None),
        ),
        check_vma=False,
    )
```

```python
import jax
import jax.numpy as jnp
from jax import lax
from jax.sharding import PartitionSpec as P


def gather_rows(own, axis_name, width):
    count = lax.axis_size(axis_name)
    me = lax.axis_index(axis_name)
    moved = [
        lax.ppermute(own, axis_name, [(i, (i + shift) % count) for i in range(count)])
        for shift in range(1, count)
    ]
    held = lax.optimization_barrier((own, *moved))
    keep = me >= 0
    fresh = lax.optimization_barrier(
        tuple(jnp.where(keep, block, jnp.zeros_like(block)) for block in held)
    )
    return [((me - shift) % count, block) for shift, block in enumerate(fresh)]


def local(tokens, cotangent, expert_ids, gate_probs, w_gate_up, w_down):
    experts = lax.axis_size("expert")
    replicas = lax.axis_size("dp")
    me_dp = lax.axis_index("dp")
    token_count = tokens.shape[0]
    model_width = tokens.shape[1]
    top_count = expert_ids.shape[1]
    hidden_units = w_down.shape[1]
    block_rows = w_gate_up.shape[1]
    capacity = 4 * token_count * top_count // (3 * experts)
    weight_blocks = gather_rows(w_gate_up[0], "dp", block_rows)
    hit = expert_ids[:, :, None] == jnp.arange(experts, dtype=jnp.int32)[None, None, :]
    token_prob = None
    for choice in range(top_count):
        term = jnp.where(hit[:, choice, :], gate_probs[:, choice : choice + 1], 0.0)
        token_prob = term if token_prob is None else token_prob + term
    token_hit = token_prob > 0.0
    earlier = (
        lax.broadcasted_iota(jnp.int32, (token_count, token_count), 0)
        > lax.broadcasted_iota(jnp.int32, (token_count, token_count), 1)
    ).astype(jnp.bfloat16)
    rank = jnp.dot(
        earlier, token_hit.astype(jnp.bfloat16), preferred_element_type=jnp.float32
    ).astype(jnp.int32)
    slot_rank = jnp.sum(jnp.where(hit, rank[:, None, :], 0), axis=2)
    target_rows = expert_ids * capacity + slot_rank
    slots = jnp.arange(experts * capacity, dtype=jnp.int32)
    chosen = token_hit.T[:, None, :] & (
        rank.T[:, None, :] == jnp.arange(capacity, dtype=jnp.int32)[None, :, None]
    )
    pick = chosen.reshape(experts * capacity, token_count).astype(jnp.bfloat16)
    slot_prob = jnp.sum(jnp.where(chosen, token_prob.T[:, None, :], 0.0), axis=2).reshape(
        experts * capacity
    )
    picked = jnp.dot(
        pick, jnp.concatenate([tokens, cotangent], axis=1), preferred_element_type=jnp.float32
    )
    columns = lax.broadcasted_iota(jnp.int32, picked.shape, 1)
    scale = jnp.where(columns < model_width, 1.0, slot_prob[:, None])
    both_send = (picked * scale).astype(jnp.bfloat16)
    both_recv = lax.all_to_all(
        both_send.reshape(experts, capacity, 2 * model_width),
        "expert",
        split_axis=0,
        concat_axis=0,
        tiled=True,
    ).reshape(experts * capacity, 2 * model_width)
    input_rows = both_recv[:, :model_width]
    cot_rows = both_recv[:, model_width:]
    weight_down = w_down[0]


    def cols(block):
        return lax.dynamic_slice_in_dim(input_rows, block * block_rows, block_rows, axis=1)

    hidden_grad = lax.dot_general(
        cot_rows, weight_down, (((1,), (1,)), ((), ())), preferred_element_type=jnp.float32
    )
    hidden_grad, held_weights = lax.optimization_barrier(
        (hidden_grad, tuple(weight for _, weight in weight_blocks))
    )
    weight_blocks = [(index, weight) for (index, _), weight in zip(weight_blocks, held_weights)]
    gate_up = None
    for block, weight in weight_blocks:
        part = jnp.dot(cols(block), weight, preferred_element_type=jnp.float32)
        gate_up = part if gate_up is None else gate_up + part
    gate = gate_up[:, :hidden_units]
    upper = gate_up[:, hidden_units:]
    sigma = jax.nn.sigmoid(gate)
    active = gate * sigma
    hidden = (active * upper).astype(jnp.bfloat16)
    output_rows = jnp.dot(hidden, weight_down, preferred_element_type=jnp.float32).astype(
        jnp.bfloat16
    )
    gate_cot = hidden_grad * upper * sigma * (1.0 + gate * (1.0 - sigma))
    upper_cot = hidden_grad * active
    pair_cot = jnp.concatenate([gate_cot, upper_cot], axis=1).astype(jnp.bfloat16)
    send_back = jnp.zeros((experts * capacity, 2 * model_width), jnp.bfloat16)
    send_back = lax.dynamic_update_slice_in_dim(send_back, output_rows, 0, axis=1)
    for block, weight in weight_blocks:
        part = lax.dot_general(
            pair_cot, weight, (((1,), (1,)), ((), ())), preferred_element_type=jnp.float32
        ).astype(jnp.bfloat16)
        send_back = lax.dynamic_update_slice_in_dim(
            send_back, part, model_width + block * block_rows, axis=1
        )
    back = lax.all_to_all(
        send_back.reshape(
            experts, capacity, 2 * model_width
        ),
        "expert",
        split_axis=0,
        concat_axis=0,
        tiled=True,
    ).reshape(experts * capacity, 2 * model_width)
    owned = (target_rows.reshape(token_count * top_count)[:, None] == slots[None, :]).astype(
        jnp.bfloat16
    )
    slot_both = jnp.dot(owned, back, preferred_element_type=jnp.float32).reshape(
        token_count, top_count, 2 * model_width
    )
    slot_out = slot_both[:, :, :model_width]
    slot_in = slot_both[:, :, model_width:]
    layer_out = jnp.sum(gate_probs[:, :, None] * slot_out, axis=1).astype(jnp.bfloat16)
    input_grad = jnp.sum(slot_in, axis=1).astype(jnp.bfloat16)
    prob_grad = jnp.sum(cotangent[:, None, :].astype(jnp.float32) * slot_out, axis=2)
    weight_cot = lax.dot_general(
        input_rows, pair_cot, (((0,), (0,)), ((), ())), preferred_element_type=jnp.float32
    )

    def grad_block(block):
        return lax.dynamic_slice_in_dim(weight_cot, block * block_rows, block_rows, axis=0)

    grad_rows = grad_block(me_dp)
    for shift in range(1, replicas):
        moved = lax.ppermute(
            grad_block((me_dp + shift) % replicas).astype(jnp.bfloat16),
            "dp",
            [(i, (i + shift) % replicas) for i in range(replicas)],
        )
        grad_rows = grad_rows + moved.astype(jnp.float32)
    return (layer_out, input_grad, prob_grad, grad_rows.astype(jnp.bfloat16)[None])


def solution(mesh):
    placed = (
        P(("dp", "expert"), None),
        P(("dp", "expert"), None),
        P(("dp", "expert"), None),
        P(("dp", "expert"), None),
        P("expert", "dp", None),
        P("expert", None, None),
    )
    return jax.shard_map(
        local,
        mesh=mesh,
        in_specs=placed,
        out_specs=(
            P(("dp", "expert"), None),
            P(("dp", "expert"), None),
            P(("dp", "expert"), None),
            P("expert", "dp", None),
        ),
        check_vma=False,
    )
```

```python
import jax
import jax.numpy as jnp
from jax import lax
from jax.sharding import PartitionSpec as P


def gather_rows(own, axis_name, width):
    count = lax.axis_size(axis_name)
    me = lax.axis_index(axis_name)
    moved = [
        lax.ppermute(own, axis_name, [(i, (i + shift) % count) for i in range(count)])
        for shift in range(1, count)
    ]
    held = lax.optimization_barrier((own, *moved))
    keep = me >= 0
    fresh = lax.optimization_barrier(
        tuple(jnp.where(keep, block, jnp.zeros_like(block)) for block in held)
    )
    return [((me - shift) % count, block) for shift, block in enumerate(fresh)]


def local(tokens, cotangent, expert_ids, gate_probs, w_gate_up, w_down):
    experts = lax.axis_size("expert")
    replicas = lax.axis_size("dp")
    me_dp = lax.axis_index("dp")
    token_count = tokens.shape[0]
    model_width = tokens.shape[1]
    top_count = expert_ids.shape[1]
    hidden_units = w_down.shape[1]
    block_rows = w_gate_up.shape[1]
    capacity = 4 * token_count * top_count // (3 * experts)
    weight_blocks = gather_rows(w_gate_up[0], "dp", block_rows)
    hit = expert_ids[:, :, None] == jnp.arange(experts, dtype=jnp.int32)[None, None, :]
    token_prob = jnp.sum(jnp.where(hit, gate_probs[:, :, None], 0.0), axis=1)
    token_hit = token_prob > 0.0
    earlier = (
        lax.broadcasted_iota(jnp.int32, (token_count, token_count), 0)
        > lax.broadcasted_iota(jnp.int32, (token_count, token_count), 1)
    ).astype(jnp.bfloat16)
    rank = jnp.dot(
        earlier, token_hit.astype(jnp.bfloat16), preferred_element_type=jnp.float32
    ).astype(jnp.int32)
    slot_rank = jnp.sum(jnp.where(hit, rank[:, None, :], 0), axis=2)
    target_rows = expert_ids * capacity + slot_rank
    slots = jnp.arange(experts * capacity, dtype=jnp.int32)
    chosen = token_hit.T[:, None, :] & (
        rank.T[:, None, :] == jnp.arange(capacity, dtype=jnp.int32)[None, :, None]
    )
    pick = chosen.reshape(experts * capacity, token_count).astype(jnp.bfloat16)
    slot_prob = jnp.sum(jnp.where(chosen, token_prob.T[:, None, :], 0.0), axis=2).reshape(
        experts * capacity
    )
    picked = jnp.dot(
        pick, jnp.concatenate([tokens, cotangent], axis=1), preferred_element_type=jnp.float32
    )
    columns = lax.broadcasted_iota(jnp.int32, picked.shape, 1)
    scale = jnp.where(columns < model_width, 1.0, slot_prob[:, None])
    both_send = (picked * scale).astype(jnp.bfloat16)
    both_recv = lax.all_to_all(
        both_send.reshape(experts, capacity, 2 * model_width),
        "expert",
        split_axis=0,
        concat_axis=0,
        tiled=True,
    ).reshape(experts * capacity, 2 * model_width)
    input_rows = both_recv[:, :model_width]
    cot_rows = both_recv[:, model_width:]
    weight_down = w_down[0]


    def cols(block):
        return lax.dynamic_slice_in_dim(input_rows, block * block_rows, block_rows, axis=1)

    hidden_grad = lax.dot_general(
        cot_rows, weight_down, (((1,), (1,)), ((), ())), preferred_element_type=jnp.float32
    )
    hidden_grad, held_weights = lax.optimization_barrier(
        (hidden_grad, tuple(weight for _, weight in weight_blocks))
    )
    weight_blocks = [(index, weight) for (index, _), weight in zip(weight_blocks, held_weights)]
    gate_up = None
    for block, weight in weight_blocks:
        part = jnp.dot(cols(block), weight, preferred_element_type=jnp.float32)
        gate_up = part if gate_up is None else gate_up + part
    gate = gate_up[:, :hidden_units]
    upper = gate_up[:, hidden_units:]
    sigma = jax.nn.sigmoid(gate)
    active = gate * sigma
    hidden = (active * upper).astype(jnp.bfloat16)
    output_rows = jnp.dot(hidden, weight_down, preferred_element_type=jnp.float32).astype(
        jnp.bfloat16
    )
    gate_cot = hidden_grad * upper * sigma * (1.0 + gate * (1.0 - sigma))
    upper_cot = hidden_grad * active
    pair_cot = jnp.concatenate([gate_cot, upper_cot], axis=1).astype(jnp.bfloat16)
    send_back = jnp.zeros((experts * capacity, 2 * model_width), jnp.bfloat16)
    send_back = lax.dynamic_update_slice_in_dim(send_back, output_rows, 0, axis=1)
    for block, weight in weight_blocks:
        part = lax.dot_general(
            pair_cot, weight, (((1,), (1,)), ((), ())), preferred_element_type=jnp.float32
        ).astype(jnp.bfloat16)
        send_back = lax.dynamic_update_slice_in_dim(
            send_back, part, model_width + block * block_rows, axis=1
        )
    back = lax.all_to_all(
        send_back.reshape(
            experts, capacity, 2 * model_width
        ),
        "expert",
        split_axis=0,
        concat_axis=0,
        tiled=True,
    ).reshape(experts * capacity, 2 * model_width)
    owned = lax.optimization_barrier(
        (target_rows.reshape(token_count * top_count)[:, None] == slots[None, :]).astype(
            jnp.bfloat16
        )
    )
    slot_both = jnp.dot(owned, back, preferred_element_type=jnp.float32).reshape(
        token_count, top_count, 2 * model_width
    )
    slot_out = slot_both[:, :, :model_width]
    slot_in = slot_both[:, :, model_width:]
    layer_out = jnp.sum(gate_probs[:, :, None] * slot_out, axis=1).astype(jnp.bfloat16)
    input_grad = jnp.sum(slot_in, axis=1).astype(jnp.bfloat16)
    prob_grad = jnp.sum(cotangent[:, None, :].astype(jnp.float32) * slot_out, axis=2)
    weight_cot = lax.dot_general(
        input_rows, pair_cot, (((0,), (0,)), ((), ())), preferred_element_type=jnp.float32
    )

    def grad_block(block):
        return lax.dynamic_slice_in_dim(weight_cot, block * block_rows, block_rows, axis=0)

    grad_rows = grad_block(me_dp)
    for shift in range(1, replicas):
        moved = lax.ppermute(
            grad_block((me_dp + shift) % replicas).astype(jnp.bfloat16),
            "dp",
            [(i, (i + shift) % replicas) for i in range(replicas)],
        )
        grad_rows = grad_rows + moved.astype(jnp.float32)
    return (layer_out, input_grad, prob_grad, grad_rows.astype(jnp.bfloat16)[None])


def solution(mesh):
    placed = (
        P(("dp", "expert"), None),
        P(("dp", "expert"), None),
        P(("dp", "expert"), None),
        P(("dp", "expert"), None),
        P("expert", "dp", None),
        P("expert", None, None),
    )
    return jax.shard_map(
        local,
        mesh=mesh,
        in_specs=placed,
        out_specs=(
            P(("dp", "expert"), None),
            P(("dp", "expert"), None),
            P(("dp", "expert"), None),
            P("expert", "dp", None),
        ),
        check_vma=False,
    )
```

```python
import jax
import jax.numpy as jnp
from jax import lax
from jax.sharding import PartitionSpec as P


def gather_rows(own, axis_name, width):
    count = lax.axis_size(axis_name)
    me = lax.axis_index(axis_name)
    moved = [
        lax.ppermute(own, axis_name, [(i, (i + shift) % count) for i in range(count)])
        for shift in range(1, count)
    ]
    held = lax.optimization_barrier((own, *moved))
    keep = me >= 0
    fresh = (held[0],) + lax.optimization_barrier(
        tuple(jnp.where(keep, block, jnp.zeros_like(block)) for block in held[1:])
    )
    return [((me - shift) % count, block) for shift, block in enumerate(fresh)]


def local(tokens, cotangent, expert_ids, gate_probs, w_gate_up, w_down):
    experts = lax.axis_size("expert")
    replicas = lax.axis_size("dp")
    me_dp = lax.axis_index("dp")
    token_count = tokens.shape[0]
    model_width = tokens.shape[1]
    top_count = expert_ids.shape[1]
    hidden_units = w_down.shape[1]
    block_rows = w_gate_up.shape[1]
    capacity = 4 * token_count * top_count // (3 * experts)
    weight_blocks = gather_rows(w_gate_up[0], "dp", block_rows)
    hit = expert_ids[:, :, None] == jnp.arange(experts, dtype=jnp.int32)[None, None, :]
    token_prob = jnp.sum(jnp.where(hit, gate_probs[:, :, None], 0.0), axis=1)
    token_hit = token_prob > 0.0
    earlier = (
        lax.broadcasted_iota(jnp.int32, (token_count, token_count), 0)
        > lax.broadcasted_iota(jnp.int32, (token_count, token_count), 1)
    ).astype(jnp.bfloat16)
    rank = jnp.dot(
        earlier, token_hit.astype(jnp.bfloat16), preferred_element_type=jnp.float32
    ).astype(jnp.int32)
    slot_rank = jnp.sum(jnp.where(hit, rank[:, None, :], 0), axis=2)
    target_rows = expert_ids * capacity + slot_rank
    slots = jnp.arange(experts * capacity, dtype=jnp.int32)
    chosen = token_hit.T[:, None, :] & (
        rank.T[:, None, :] == jnp.arange(capacity, dtype=jnp.int32)[None, :, None]
    )
    pick = chosen.reshape(experts * capacity, token_count).astype(jnp.bfloat16)
    slot_prob = jnp.sum(jnp.where(chosen, token_prob.T[:, None, :], 0.0), axis=2).reshape(
        experts * capacity
    )
    picked = jnp.dot(
        pick, jnp.concatenate([tokens, cotangent], axis=1), preferred_element_type=jnp.float32
    )
    columns = lax.broadcasted_iota(jnp.int32, picked.shape, 1)
    scale = jnp.where(columns < model_width, 1.0, slot_prob[:, None])
    both_send = (picked * scale).astype(jnp.bfloat16)
    both_recv = lax.all_to_all(
        both_send.reshape(experts, capacity, 2 * model_width),
        "expert",
        split_axis=0,
        concat_axis=0,
        tiled=True,
    ).reshape(experts * capacity, 2 * model_width)
    input_rows = both_recv[:, :model_width]
    cot_rows = both_recv[:, model_width:]
    weight_down = w_down[0]


    def cols(block):
        return lax.dynamic_slice_in_dim(input_rows, block * block_rows, block_rows, axis=1)

    hidden_grad = lax.dot_general(
        cot_rows, weight_down, (((1,), (1,)), ((), ())), preferred_element_type=jnp.float32
    )
    hidden_grad, held_weights = lax.optimization_barrier(
        (hidden_grad, tuple(weight for _, weight in weight_blocks))
    )
    weight_blocks = [(index, weight) for (index, _), weight in zip(weight_blocks, held_weights)]
    gate_up = None
    for block, weight in weight_blocks:
        part = jnp.dot(cols(block), weight, preferred_element_type=jnp.float32)
        gate_up = part if gate_up is None else gate_up + part
    gate = gate_up[:, :hidden_units]
    upper = gate_up[:, hidden_units:]
    sigma = jax.nn.sigmoid(gate)
    active = gate * sigma
    hidden = (active * upper).astype(jnp.bfloat16)
    output_rows = jnp.dot(hidden, weight_down, preferred_element_type=jnp.float32).astype(
        jnp.bfloat16
    )
    gate_cot = hidden_grad * upper * sigma * (1.0 + gate * (1.0 - sigma))
    upper_cot = hidden_grad * active
    pair_cot = jnp.concatenate([gate_cot, upper_cot], axis=1).astype(jnp.bfloat16)
    send_back = jnp.zeros((experts * capacity, 2 * model_width), jnp.bfloat16)
    send_back = lax.dynamic_update_slice_in_dim(send_back, output_rows, 0, axis=1)
    for block, weight in weight_blocks:
        part = lax.dot_general(
            pair_cot, weight, (((1,), (1,)), ((), ())), preferred_element_type=jnp.float32
        ).astype(jnp.bfloat16)
        send_back = lax.dynamic_update_slice_in_dim(
            send_back, part, model_width + block * block_rows, axis=1
        )
    back = lax.all_to_all(
        send_back.reshape(
            experts, capacity, 2 * model_width
        ),
        "expert",
        split_axis=0,
        concat_axis=0,
        tiled=True,
    ).reshape(experts * capacity, 2 * model_width)
    owned = (target_rows.reshape(token_count * top_count)[:, None] == slots[None, :]).astype(
        jnp.bfloat16
    )
    slot_both = jnp.dot(owned, back, preferred_element_type=jnp.float32).reshape(
        token_count, top_count, 2 * model_width
    )
    slot_out = slot_both[:, :, :model_width]
    slot_in = slot_both[:, :, model_width:]
    layer_out = jnp.sum(gate_probs[:, :, None] * slot_out, axis=1).astype(jnp.bfloat16)
    input_grad = jnp.sum(slot_in, axis=1).astype(jnp.bfloat16)
    prob_grad = jnp.sum(cotangent[:, None, :].astype(jnp.float32) * slot_out, axis=2)
    weight_cot = lax.dot_general(
        input_rows, pair_cot, (((0,), (0,)), ((), ())), preferred_element_type=jnp.float32
    )

    def grad_block(block):
        return lax.dynamic_slice_in_dim(weight_cot, block * block_rows, block_rows, axis=0)

    grad_rows = grad_block(me_dp)
    for shift in range(1, replicas):
        moved = lax.ppermute(
            grad_block((me_dp + shift) % replicas).astype(jnp.bfloat16),
            "dp",
            [(i, (i + shift) % replicas) for i in range(replicas)],
        )
        grad_rows = grad_rows + moved.astype(jnp.float32)
    return (layer_out, input_grad, prob_grad, grad_rows.astype(jnp.bfloat16)[None])


def solution(mesh):
    placed = (
        P(("dp", "expert"), None),
        P(("dp", "expert"), None),
        P(("dp", "expert"), None),
        P(("dp", "expert"), None),
        P("expert", "dp", None),
        P("expert", None, None),
    )
    return jax.shard_map(
        local,
        mesh=mesh,
        in_specs=placed,
        out_specs=(
            P(("dp", "expert"), None),
            P(("dp", "expert"), None),
            P(("dp", "expert"), None),
            P("expert", "dp", None),
        ),
        check_vma=False,
    )
```

```python
import jax
import jax.numpy as jnp
from jax import lax
from jax.sharding import PartitionSpec as P


def gather_rows(own, axis_name, width):
    count = lax.axis_size(axis_name)
    me = lax.axis_index(axis_name)
    moved = [
        lax.ppermute(own, axis_name, [(i, (i + shift) % count) for i in range(count)])
        for shift in range(1, count)
    ]
    held = lax.optimization_barrier((own, *moved))
    keep = me >= 0
    fresh = lax.optimization_barrier(
        tuple(jnp.where(keep, block, jnp.zeros_like(block)) for block in held)
    )
    return [((me - shift) % count, block) for shift, block in enumerate(fresh)]


def local(tokens, cotangent, expert_ids, gate_probs, w_gate_up, w_down):
    experts = lax.axis_size("expert")
    replicas = lax.axis_size("dp")
    me_dp = lax.axis_index("dp")
    token_count = tokens.shape[0]
    model_width = tokens.shape[1]
    top_count = expert_ids.shape[1]
    hidden_units = w_down.shape[1]
    block_rows = w_gate_up.shape[1]
    capacity = 4 * token_count * top_count // (3 * experts)
    weight_blocks = gather_rows(w_gate_up[0], "dp", block_rows)
    hit = expert_ids[:, :, None] == jnp.arange(experts, dtype=jnp.int32)[None, None, :]
    token_prob = jnp.sum(jnp.where(hit, gate_probs[:, :, None], 0.0), axis=1)
    token_hit = token_prob > 0.0
    earlier = (
        lax.broadcasted_iota(jnp.int32, (token_count, token_count), 0)
        > lax.broadcasted_iota(jnp.int32, (token_count, token_count), 1)
    ).astype(jnp.bfloat16)
    rank = jnp.dot(
        earlier, token_hit.astype(jnp.bfloat16), preferred_element_type=jnp.float32
    ).astype(jnp.int32)
    slot_rank = jnp.sum(jnp.where(hit, rank[:, None, :], 0), axis=2)
    target_rows = expert_ids * capacity + slot_rank
    slots = jnp.arange(experts * capacity, dtype=jnp.int32)
    chosen = token_hit.T[:, None, :] & (
        rank.T[:, None, :] == jnp.arange(capacity, dtype=jnp.int32)[None, :, None]
    )
    pick = chosen.reshape(experts * capacity, token_count).astype(jnp.bfloat16)
    slot_prob = jnp.sum(jnp.where(chosen, token_prob.T[:, None, :], 0.0), axis=2).reshape(
        experts * capacity
    )
    picked = jnp.dot(
        pick, jnp.concatenate([tokens, cotangent], axis=1), preferred_element_type=jnp.float32
    )
    columns = lax.broadcasted_iota(jnp.int32, picked.shape, 1)
    scale = jnp.where(columns < model_width, 1.0, slot_prob[:, None])
    both_send = (picked * scale).astype(jnp.bfloat16)
    both_recv = lax.all_to_all(
        both_send.reshape(experts, capacity, 2 * model_width),
        "expert",
        split_axis=0,
        concat_axis=0,
        tiled=True,
    ).reshape(experts * capacity, 2 * model_width)
    input_rows = both_recv[:, :model_width]
    cot_rows = both_recv[:, model_width:]
    weight_down = w_down[0]


    def cols(block):
        return lax.dynamic_slice_in_dim(input_rows, block * block_rows, block_rows, axis=1)

    hidden_grad = lax.dot_general(
        cot_rows, weight_down, (((1,), (1,)), ((), ())), preferred_element_type=jnp.float32
    )
    hidden_grad, held_weights = lax.optimization_barrier(
        (hidden_grad, tuple(weight for _, weight in weight_blocks))
    )
    weight_blocks = [(index, weight) for (index, _), weight in zip(weight_blocks, held_weights)]
    gate_up = None
    for block, weight in weight_blocks:
        part = jnp.dot(cols(block), weight, preferred_element_type=jnp.float32)
        gate_up = part if gate_up is None else gate_up + part
    gate = gate_up[:, :hidden_units]
    upper = gate_up[:, hidden_units:]
    sigma = jax.nn.sigmoid(gate)
    active = gate * sigma
    hidden = (active * upper).astype(jnp.bfloat16)
    output_rows = jnp.dot(hidden, weight_down, preferred_element_type=jnp.float32).astype(
        jnp.bfloat16
    )
    gate_cot = hidden_grad * upper * sigma * (1.0 + gate * (1.0 - sigma))
    upper_cot = hidden_grad * active
    pair_cot = jnp.concatenate([gate_cot, upper_cot], axis=1).astype(jnp.bfloat16)
    send_back = jnp.zeros((experts * capacity, 2 * model_width), jnp.bfloat16)
    send_back = lax.dynamic_update_slice_in_dim(send_back, output_rows, 0, axis=1)
    for block, weight in weight_blocks:
        part = lax.dot_general(
            pair_cot, weight, (((1,), (1,)), ((), ())), preferred_element_type=jnp.float32
        ).astype(jnp.bfloat16)
        send_back = lax.dynamic_update_slice_in_dim(
            send_back, part, model_width + block * block_rows, axis=1
        )
    back = lax.all_to_all(
        send_back.reshape(
            experts, capacity, 2 * model_width
        ),
        "expert",
        split_axis=0,
        concat_axis=0,
        tiled=True,
    ).reshape(experts * capacity, 2 * model_width)
    owned = (target_rows.reshape(token_count * top_count)[:, None] == slots[None, :]).astype(
        jnp.bfloat16
    )
    slot_both = jnp.dot(owned, back, preferred_element_type=jnp.float32).reshape(
        token_count, top_count, 2 * model_width
    )
    slot_out = slot_both[:, :, :model_width]
    slot_in = slot_both[:, :, model_width:]
    layer_out = jnp.sum(gate_probs[:, :, None] * slot_out, axis=1).astype(jnp.bfloat16)
    input_grad = jnp.sum(slot_in, axis=1).astype(jnp.bfloat16)
    prob_grad = jnp.sum(cotangent[:, None, :].astype(jnp.float32) * slot_out, axis=2)
    weight_cot = lax.dot_general(
        input_rows, pair_cot, (((0,), (0,)), ((), ())), preferred_element_type=jnp.float32
    )

    def grad_block(block):
        return lax.dynamic_slice_in_dim(weight_cot, block * block_rows, block_rows, axis=0)

    grad_rows = grad_block(me_dp).astype(jnp.bfloat16).astype(jnp.float32)
    for shift in range(1, replicas):
        moved = lax.ppermute(
            grad_block((me_dp + shift) % replicas).astype(jnp.bfloat16),
            "dp",
            [(i, (i + shift) % replicas) for i in range(replicas)],
        )
        grad_rows = grad_rows + moved.astype(jnp.float32)
    return (layer_out, input_grad, prob_grad, grad_rows.astype(jnp.bfloat16)[None])


def solution(mesh):
    placed = (
        P(("dp", "expert"), None),
        P(("dp", "expert"), None),
        P(("dp", "expert"), None),
        P(("dp", "expert"), None),
        P("expert", "dp", None),
        P("expert", None, None),
    )
    return jax.shard_map(
        local,
        mesh=mesh,
        in_specs=placed,
        out_specs=(
            P(("dp", "expert"), None),
            P(("dp", "expert"), None),
            P(("dp", "expert"), None),
            P("expert", "dp", None),
        ),
        check_vma=False,
    )
```
